128 devices in a mesh: row: 16 (over x, z), col: 8 (over y, core).
Axes of the slice: x: 4, y: 4, z: 4, core: 2. Of those that a mesh axis runs over, the one named last changes fastest.
Arguments:
- a_vals: float32 [16, 8, 448, 4096], P('row', 'col'), may hold values from -0.1875 to 0.1875
- a_row: int32 [16, 8, 448], P('row', 'col'), may hold values from 0 to 63
- a_col: int32 [16, 8, 448], P('row', 'col'), may hold values from 0 to 127
- a_slot: int32 [16, 8, 3, 448], P('row', 'col'), may hold values from 0 to 5
- a_count: int32 [16, 8], P('row', 'col'), may hold values from 1 to 448, as said below
- p_vals: float32 [1024, 3, 4096], P(('row', 'col')), may hold values from -0.75 to 0.75
- p_owner: int32 [1024, 3], P(('row', 'col')), may hold values from 0 to 15, all different within a row; in each aligned block of 8 rows (0 to 7, 8 to 15, ...) at most 2 rows name the same one
- p_sub: int32 [1024, 3], P(('row', 'col')), may hold values from 0 to 7
- ap_cslot: int32 [1024, 3, 6], P(('row', 'col')), may hold values from 0 to 26
Outputs:
- coarse: float32 [128, 27, 4096], P(('row', 'col'))
The draws below stay inside these ranges and needn't reach their ends.
Inputs may be any that keep to these rules, and one draw needn't show every extreme that they name: `a_count`: at least one device holds exactly 448 listed blocks. `p_owner`: the 3 entries of a fine block row differ; among the rows of one device each row group is named at most 2 times.
All inputs are finite; a program needn't handle non-finite values.
Results may differ from the reference program's by a relative error of at most 0.0001.
Values sent between devices are 32-bit elements; how exact they have to be, the bound alone decides.
No kernel may reach another device: no remote copies, remote signals or barrier semaphores. Data moves between devices by JAX's collectives and lax.ppermute only.
A program may use at most 128 MiB of HBM per device.

```python
import math
import jax
import jax.numpy as jnp
import numpy as np
from jax import lax

BLOCK = 64
TILE = 4096
RPD = 8
TP = 3
TAP = 6
TC = 27
TA = 448
RG = 64
CG = 128
NB = 1024
CRG = 8
NC = 128
CAPR = 2
N_ROW = 16
N_COL = 8


def draw_a_count(key, part):
    key_levels, key_pick, key_jitter = jax.random.split(key, 3)
    devices_all = N_ROW * N_COL
    levels = jax.random.randint(key_levels, (devices_all,), 1, 5)
    weights = levels * levels
    chosen = jax.random.randint(key_pick, (), 0, devices_all)
    marked = jnp.arange(devices_all) == chosen
    weights = jnp.where(marked, 16, weights)
    jitter = jax.random.randint(key_jitter, (devices_all,), 0, TA // 32 + 1)
    jitter = jnp.where(marked, 0, jitter)
    counts = jnp.maximum(TA * weights // 16 - jitter, 1)
    return counts.reshape(N_ROW, N_COL).astype(jnp.int32)


def plant(drawn, own_key, smallest, high):
    place = [jax.random.randint(jax.random.fold_in(own_key, axis), (), 0, length) for axis, length in enumerate(drawn.shape)]
    widest = drawn.shape.index(max(drawn.shape))
    next_to = place[:widest] + [(place[widest] + 1) % drawn.shape[widest]] + place[widest + 1:]
    return drawn.at[tuple(place)].set(smallest).at[tuple(next_to)].set(high)


def block_levels(key, shape, cuts, smallest, top_value):
    factor_of, own = 1.0, jax.random.fold_in(key, 6)
    for dim, shards_of in cuts:
        draws = jnp.exp(jax.random.uniform(jax.random.fold_in(own, dim), (shards_of,), jnp.float32, smallest / len(cuts), top_value / len(cuts)))
        factor_of = factor_of * jnp.repeat(draws, shape[dim] // shards_of).reshape([-1 if axis == dim else 1 for axis in range(len(shape))])
    return factor_of


def deal_out(stream_key, own, number, rows, number_of, top, most, skew):
    order = jax.random.permutation(stream_key, number_of)
    heavy_load, common = shares(number_of, rows * top, most, skew, True), shares(number_of, rows * top, most, skew, False)
    places = jnp.arange(number_of)

    def named(lengths, offset_by):
        used = int((lengths > 0).sum())
        fixed = max(1, used // 4)
        passed = fixed + (places - fixed + offset_by * (used - fixed)) % max(1, number_of - fixed)
        return jnp.zeros((number_of,), jnp.int32).at[order[jnp.where(places < fixed, places, passed)]].set(jnp.asarray(lengths, jnp.int32))

    lengths = jnp.where(number % 4 == 0, named(heavy_load, number // 4), named(common, number - number // 4 - 1))
    mixed = jax.random.permutation(jax.random.fold_in(own, 3), number_of)
    donor, taker = mixed[0:number_of // 2 * 2:2], mixed[1:number_of // 2 * 2:2]
    margin = jnp.minimum(lengths[donor] - 1, most - lengths[taker]) // 2
    margin = jnp.where((donor == order[0]) | (taker == order[0]) | (lengths[taker] == 0), 0, jnp.maximum(margin, 0))
    passed = jax.random.randint(jax.random.fold_in(own, 4), (number_of // 2,), 0, 1 << 20) % (margin + 1)
    lengths = lengths.at[donor].add(-passed).at[taker].add(passed)
    labels = jnp.searchsorted(jnp.cumsum(lengths), jnp.arange(rows * top), side="right").astype(jnp.int32)
    listing = labels.reshape(top, rows).T
    listing = listing[jax.random.permutation(jax.random.fold_in(own, 1), rows)]
    offset_by = jax.random.randint(jax.random.fold_in(own, 2), (rows, 1), 0, top)
    return jnp.take_along_axis(listing, (jnp.arange(top)[None, :] + offset_by) % top, axis=1)


def shares(amount, total, most, slope, full):
    portions = [(1 << 20) // math.isqrt(rank ** slope) + 1 for rank in range(1, amount + 1)]
    largest = most if full else min(most, max(-(-total // amount), total * portions[0] // sum(portions)))
    least = 1 if total - largest >= amount - 1 else 0
    given, surplus = [largest] + [least] * (amount - 1), total - largest - least * (amount - 1)
    while surplus > 0:
        candidates = [i for i in range(1, amount) if given[i] < largest] or [i for i in range(1, amount) if given[i] < most]
        mass, budget = sum([portions[i] for i in candidates]), surplus
        for i in candidates:
            more = min(most - given[i], max(1, budget * portions[i] // mass), surplus)
            given[i] = given[i] + more
            surplus = surplus - more
    return np.array(given)


def centred(own_key, dims, scale, reach, cuts=(), kind=jnp.bfloat16):
    result = scale * jax.random.normal(own_key, dims, jnp.float32)
    if cuts:
        result = result * block_levels(own_key, dims, cuts, -0.22, 0.18)
    return jnp.clip(result, -reach, reach).astype(kind)


def setup_inputs(seed: int = 0) -> dict:
    key_of = jax.random.split(jax.random.key(seed), 10)
    a_vals = centred(key_of[0], (N_ROW, N_COL, TA, TILE), (BLOCK * 16) ** -0.5, 0.1875, ((0, 16), (1, 8)), jnp.float32)
    a_row = plant(jax.random.randint(key_of[1], (N_ROW, N_COL, TA), 0, RG), jax.random.fold_in(key_of[1], 1), 0, RG - 1).astype(jnp.int32)
    a_col = plant(jax.random.randint(key_of[2], (N_ROW, N_COL, TA), 0, CG), jax.random.fold_in(key_of[2], 1), 0, CG - 1).astype(jnp.int32)
    a_slot = plant(jax.random.randint(key_of[3], (N_ROW, N_COL, TP, TA), 0, TAP), jax.random.fold_in(key_of[3], 1), 0, TAP - 1).astype(jnp.int32)
    a_count = draw_a_count(jax.random.fold_in(key_of[9], 71), 0)
    p_vals = centred(key_of[5], (NB, TP, TILE), BLOCK ** -0.5, 0.75, ((0, 128),), jnp.float32)
    p_owner_keys = jax.random.split(jax.random.fold_in(key_of[6], 1), NB // RPD)
    p_owner_turns = jax.random.permutation(jax.random.fold_in(key_of[6], 3), NB // RPD)
    p_owner = jax.vmap(lambda own, number: deal_out(jax.random.fold_in(key_of[6], 2), own, number, RPD, N_ROW, TP, CAPR, 1))(p_owner_keys, p_owner_turns).reshape((NB, TP))
    p_sub = plant(jax.random.randint(key_of[7], (NB, TP), 0, CRG), jax.random.fold_in(key_of[7], 1), 0, CRG - 1).astype(jnp.int32)
    ap_cslot = plant(jax.random.randint(key_of[8], (NB, TP, TAP), 0, TC), jax.random.fold_in(key_of[8], 1), 0, TC - 1).astype(jnp.int32)
    return dict(a_vals=a_vals, a_row=a_row, a_col=a_col, a_slot=a_slot, a_count=a_count, p_vals=p_vals, p_owner=p_owner, p_sub=p_sub, ap_cslot=ap_cslot)


highest = lax.Precision.HIGHEST


def reference(a_vals, a_row, a_col, a_slot, a_count, p_vals, p_owner, p_sub, ap_cslot):
    devices_all = N_ROW * N_COL
    tiles_flat = a_vals.reshape(devices_all, TA, BLOCK, BLOCK)
    rows_flat = a_row.reshape(devices_all, TA).astype(jnp.int32)
    cols_flat = a_col.reshape(devices_all, TA).astype(jnp.int32)
    slots_flat = a_slot.reshape(devices_all, TP, TA).astype(jnp.int32)
    counts_flat = a_count.reshape(devices_all).astype(jnp.int32)
    prolong = p_vals.reshape(NB, TP, BLOCK, BLOCK)

    def add_device(device, product_sum):
        row_group = device // N_COL
        col_group = device % N_COL
        matrix_tiles = lax.dynamic_index_in_dim(tiles_flat, device, 0, False)
        tile_rows = lax.dynamic_index_in_dim(rows_flat, device, 0, False)
        tile_cols = lax.dynamic_index_in_dim(cols_flat, device, 0, False)
        tile_slots = lax.dynamic_index_in_dim(slots_flat, device, 0, False)
        tile_count = lax.dynamic_index_in_dim(counts_flat, device, 0, False)
        fine_col = (tile_cols // RPD) * RG + col_group * RPD + tile_cols % RPD
        right_tiles = jnp.take(prolong, fine_col.astype(jnp.int32), axis=0)
        products = jnp.einsum("tij,tsjk->tsik", matrix_tiles, right_tiles, precision=highest)
        is_live = jnp.arange(TA, dtype=jnp.int32) < tile_count
        products = jnp.where(is_live[:, None, None, None], products, jnp.zeros_like(products))
        target = (row_group * RG + tile_rows)[:, None] * TAP + tile_slots.T
        return product_sum.at[target.reshape(-1).astype(jnp.int32)].add(products.reshape(TA * TP, TILE))

    product_sum = lax.fori_loop(0, devices_all, add_device, jnp.zeros((NB * TAP, TILE), jnp.float32))
    ap_tiles = product_sum.reshape(NB, TAP, BLOCK, BLOCK)
    coarse_row = p_owner.astype(jnp.int32) * CRG + p_sub.astype(jnp.int32)
    cslots = ap_cslot.astype(jnp.int32)
    coarse_sum = jnp.zeros((NC * TC, TILE), jnp.float32)
    for branch in range(TP):
        left_tiles = prolong[:, branch]
        contribs = jnp.einsum("ijk,iqjl->iqkl", left_tiles, ap_tiles, precision=highest)
        target = coarse_row[:, branch][:, None] * TC + cslots[:, branch, :]
        coarse_sum = coarse_sum.at[target.reshape(-1).astype(jnp.int32)].add(contribs.reshape(NB * TAP, TILE))
    return coarse_sum.reshape(NC, TC, TILE)
```

```python
import functools

import jax
import jax.numpy as jnp
from jax import lax
from jax.experimental import pallas as pl
from jax.experimental.pallas import tpu as pltpu
from jax.sharding import PartitionSpec as P

BLOCK = 64
CPD = 1
TAP = 6
TC = 27


highest = lax.Precision.HIGHEST
chunk = 32


def ap_kernel(rows_ref, cols_ref, slots_ref, cnt_ref, a_ref, p_ref, o_ref):
    c = pl.program_id(0)
    capacity = rows_ref.shape[0]
    branches = p_ref.shape[1]

    @pl.when(c == 0)
    def _():
        o_ref[...] = jnp.zeros(o_ref.shape, o_ref.dtype)

    count = cnt_ref[0]

    def body(u, carry):
        t = c * chunk + u

        @pl.when(t < count)
        def _():
            a = a_ref[u]
            col = cols_ref[t]
            row = rows_ref[t]
            for s in range(branches):
                prod = jnp.dot(
                    a, p_ref[col, s], preferred_element_type=jnp.float32, precision=highest
                )
                idx = row * TAP + slots_ref[s * capacity + t]
                o_ref[idx] += prod

        return carry

    lax.fori_loop(0, chunk, body, 0)


def ap_partial(tiles, rows, cols, slots, count, panel, out_rows):
    capacity = tiles.shape[0]
    chunks = capacity // chunk

    def a_map(c, rows_ref, cols_ref, slots_ref, cnt_ref):
        last = (cnt_ref[0] - 1) // chunk
        return (jnp.minimum(c, last), 0, 0)

    grid_spec = pltpu.PrefetchScalarGridSpec(
        num_scalar_prefetch=4,
        grid=(chunks,),
        in_specs=[
            pl.BlockSpec((chunk, BLOCK, BLOCK), a_map),
            pl.BlockSpec(memory_space=pltpu.VMEM),
        ],
        out_specs=pl.BlockSpec(memory_space=pltpu.VMEM),
    )
    return pl.pallas_call(
        ap_kernel,
        out_shape=jax.ShapeDtypeStruct((out_rows * TAP, BLOCK, BLOCK), jnp.float32),
        grid_spec=grid_spec,
        compiler_params=pltpu.CompilerParams(
            dimension_semantics=("arbitrary",), vmem_limit_bytes=56 * 1024 * 1024
        ),
    )(rows, cols, slots, count, tiles, panel)


def on_device(a_vals, a_row, a_col, a_slot, a_count, p_vals, p_owner, p_sub, ap_cslot):
    row_devices = lax.axis_size("row")
    col_devices = lax.axis_size("col")
    capacity = a_vals.shape[2]
    rows_dev = p_vals.shape[0]
    branches = p_vals.shape[1]
    tile_len = p_vals.shape[2]
    group_rows = rows_dev * col_devices
    group_coarse = CPD * col_devices
    per_peer = max(2, 3 * rows_dev * branches // (2 * row_devices))
    matrix_tiles = a_vals.reshape(capacity, BLOCK, BLOCK)
    tile_rows = a_row.reshape(capacity)
    tile_cols = a_col.reshape(capacity)
    tile_slots = a_slot.reshape(branches * capacity)
    tile_count = a_count.reshape(1)
    panel = lax.all_gather(p_vals, "row", axis=0, tiled=True)
    panel_tiles = panel.reshape(rows_dev * row_devices, branches, BLOCK, BLOCK)

    partial_value = ap_partial(
        matrix_tiles, tile_rows, tile_cols, tile_slots, tile_count, panel_tiles, group_rows
    )
    ap_rows = lax.psum_scatter(
        partial_value.reshape(group_rows, TAP, tile_len), "col", scatter_dimension=0, tiled=True
    )
    item_count = rows_dev * branches
    owners = p_owner.reshape(item_count)
    serial = jnp.arange(item_count, dtype=jnp.int32)
    earlier = (owners[:, None] == owners[None, :]) & (serial[None, :] < serial[:, None])
    placed = owners * per_peer + jnp.sum(earlier.astype(jnp.int32), axis=1)
    slots_total = row_devices * per_peer
    metadata = jnp.concatenate(
        [p_sub.reshape(item_count, 1), ap_cslot.reshape(item_count, TAP)], axis=1
    ).astype(jnp.float32)
    meta_send = jnp.zeros((slots_total, TAP + 1), jnp.float32).at[placed].set(metadata)
    ap_items = jnp.broadcast_to(ap_rows[:, None], (rows_dev, branches, TAP, tile_len)).reshape(
        item_count, TAP, tile_len
    )
    packed = jnp.concatenate([p_vals.reshape(item_count, 1, tile_len), ap_items], axis=1)
    outgoing = jnp.zeros((slots_total, TAP + 1, tile_len), jnp.float32).at[placed].set(packed)
    incoming, meta_in = (
        lax.all_to_all(outgoing, "row", split_axis=0, concat_axis=0, tiled=True),
        lax.all_to_all(meta_send, "row", split_axis=0, concat_axis=0, tiled=True),
    )
    left_in = incoming[:, 0].reshape(slots_total, BLOCK, BLOCK)
    right_in = incoming[:, 1:].reshape(slots_total, TAP, BLOCK, BLOCK)
    arrived = jnp.einsum("ejk,eqjl->eqkl", left_in, right_in, precision=highest).reshape(
        slots_total, TAP, tile_len
    )
    arrived_index = meta_in.astype(jnp.int32)
    target = arrived_index[:, :1] * TC + arrived_index[:, 1:]
    coarse_part = (
        jnp.zeros((group_coarse * TC, tile_len), jnp.float32)
        .at[target.reshape(-1)]
        .add(arrived.reshape(slots_total * TAP, tile_len))
    )
    coarse = lax.psum_scatter(
        coarse_part.reshape(group_coarse, TC, tile_len), "col", scatter_dimension=0, tiled=True
    )
    return coarse


def solution(mesh):
    placed = (
        P("row", "col", None, None),
        P("row", "col", None),
        P("row", "col", None),
        P("row", "col", None, None),
        P("row", "col"),
        P(("row", "col"), None, None),
        P(("row", "col"), None),
        P(("row", "col"), None),
        P(("row", "col"), None, None),
    )
    return jax.shard_map(
        on_device,
        mesh=mesh,
        in_specs=placed,
        out_specs=P(("row", "col"), None, None),
        check_vma=False,
    )
```

```python
import jax
import jax.numpy as jnp
from jax import lax
from jax.experimental import pallas as pl
from jax.experimental.pallas import tpu as pltpu
from jax.sharding import PartitionSpec as P

BLOCK = 64
TAP = 6
TC = 27
LANES = 128
HALF = BLOCK * BLOCK // LANES

highest = lax.Precision.HIGHEST
chunk = 32


def ap_kernel(rows_ref, cols_ref, slots_ref, cnt_ref, a_ref, p_ref, o_ref):
    c = pl.program_id(0)
    capacity = rows_ref.shape[0]
    branches = p_ref.shape[2] // LANES

    @pl.when(c == 0)
    def _():
        o_ref[...] = jnp.zeros(o_ref.shape, o_ref.dtype)

    count = cnt_ref[0]

    def body(u, carry):
        t = c * chunk + u

        @pl.when(t < count)
        def _():
            col = cols_ref[t]
            row = rows_ref[t]
            prod = jnp.dot(
                a_ref[u], p_ref[col], preferred_element_type=jnp.float32, precision=highest
            )
            for s in range(branches):
                idx = row * TAP + slots_ref[s * capacity + t]
                o_ref[idx] += prod[:, s * LANES:(s + 1) * LANES]

        return carry

    lax.fori_loop(0, chunk, body, 0)


def ap_partial(tiles, rows, cols, slots, count, pdiag, out_rows):
    capacity = tiles.shape[0]
    chunks = capacity // chunk

    def a_map(c, rows_ref, cols_ref, slots_ref, cnt_ref):
        last = (cnt_ref[0] - 1) // chunk
        return (jnp.minimum(c, last), 0, 0)

    grid_spec = pltpu.PrefetchScalarGridSpec(
        num_scalar_prefetch=4,
        grid=(chunks,),
        in_specs=[
            pl.BlockSpec((chunk, HALF, LANES), a_map),
            pl.BlockSpec(memory_space=pltpu.VMEM),
        ],
        out_specs=pl.BlockSpec(memory_space=pltpu.VMEM),
    )
    return pl.pallas_call(
        ap_kernel,
        out_shape=jax.ShapeDtypeStruct((out_rows * TAP, HALF, LANES), jnp.float32),
        grid_spec=grid_spec,
        compiler_params=pltpu.CompilerParams(
            dimension_semantics=("arbitrary",), vmem_limit_bytes=60 * 1024 * 1024
        ),
    )(rows, cols, slots, count, tiles, pdiag)


def block_diagonal(panel):
    cols, branches = panel.shape[:2]
    p4 = panel.reshape(cols, branches, BLOCK, BLOCK)
    zero = jnp.zeros_like(p4)
    top = jnp.concatenate([p4, zero], axis=3)
    bottom = jnp.concatenate([zero, p4], axis=3)
    both = jnp.concatenate([top, bottom], axis=2)
    return both.transpose(0, 2, 1, 3).reshape(cols, 2 * BLOCK, branches * LANES)


def on_device(a_vals, a_row, a_col, a_slot, a_count, p_vals, p_owner, p_sub, ap_cslot):
    row_devices = lax.axis_size("row")
    col_devices = lax.axis_size("col")
    capacity = a_vals.shape[2]
    rows_dev = p_vals.shape[0]
    branches = p_vals.shape[1]
    tile_len = p_vals.shape[2]
    group_rows = rows_dev * col_devices
    per_peer = 2
    item_count = rows_dev * branches
    slots_total = row_devices * per_peer

    meta_local = jnp.concatenate(
        [p_owner.reshape(item_count, 1), p_sub.reshape(item_count, 1),
         ap_cslot.reshape(item_count, TAP)], axis=1
    ).astype(jnp.float32)
    meta_all = lax.all_gather(meta_local, "row", axis=0, tiled=False)

    panel = lax.all_gather(p_vals, "row", axis=0, tiled=True)
    pdiag = block_diagonal(panel)
    matrix_tiles = a_vals.reshape(capacity, HALF, LANES)
    partial_value = ap_partial(
        matrix_tiles, a_row.reshape(capacity), a_col.reshape(capacity),
        a_slot.reshape(branches * capacity), a_count.reshape(1), pdiag, group_rows
    )
    ap_rows = lax.psum_scatter(
        partial_value.reshape(group_rows, TAP, HALF, LANES), "col", scatter_dimension=0, tiled=True
    )

    p4 = p_vals.reshape(rows_dev, branches, BLOCK, BLOCK)
    ap4 = ap_rows.reshape(rows_dev, TAP, BLOCK, BLOCK)
    prods = jnp.einsum("isjk,iqjl->isqkl", p4, ap4, precision=highest)
    prods = prods.reshape(item_count, TAP, tile_len)
    prods = jnp.concatenate([prods, jnp.zeros((1, TAP, tile_len), jnp.float32)], axis=0)

    owners = p_owner.reshape(item_count)
    serial = jnp.arange(item_count, dtype=jnp.int32)
    earlier = (owners[:, None] == owners[None, :]) & (serial[None, :] < serial[:, None])
    placed = owners * per_peer + jnp.sum(earlier.astype(jnp.int32), axis=1)
    slot_ids = jnp.arange(slots_total, dtype=jnp.int32)
    hit = placed[None, :] == slot_ids[:, None]
    source = jnp.where(
        jnp.any(hit, axis=1), jnp.sum(jnp.where(hit, serial[None, :], 0), axis=1), item_count
    )
    outgoing = jnp.take(prods, source, axis=0)
    incoming = lax.all_to_all(outgoing, "row", split_axis=0, concat_axis=0, tiled=True)

    me = lax.axis_index("row").astype(jnp.float32)
    meta_all = meta_all.reshape(row_devices, item_count, TAP + 2)
    match = meta_all[:, :, 0] == me
    rank = jnp.cumsum(match.astype(jnp.int32), axis=1) - 1
    ranks = jnp.arange(per_peer, dtype=jnp.int32)
    pick = match[:, None, :] & (rank[:, None, :] == ranks[None, :, None])
    dest = meta_all[:, :, 1:2] * TC + meta_all[:, :, 2:]
    dest_slot = jnp.sum(jnp.where(pick[..., None], dest[:, None, :, :], 0.0), axis=2)
    valid = jnp.any(pick, axis=2)
    dest_slot = jnp.where(valid[..., None], dest_slot, -1.0).reshape(slots_total * TAP)
    group_coarse = col_devices * TC
    onehot = (
        dest_slot[:, None] == jnp.arange(group_coarse, dtype=jnp.float32)[None, :]
    ).astype(jnp.float32)
    coarse_part = jnp.einsum(
        "ec,ef->cf", onehot, incoming.reshape(slots_total * TAP, tile_len), precision=highest
    )
    coarse = lax.psum_scatter(
        coarse_part.reshape(col_devices, TC, tile_len), "col", scatter_dimension=0, tiled=True
    )
    return coarse


def solution(mesh):
    placed = (
        P("row", "col", None, None),
        P("row", "col", None),
        P("row", "col", None),
        P("row", "col", None, None),
        P("row", "col"),
        P(("row", "col"), None, None),
        P(("row", "col"), None),
        P(("row", "col"), None),
        P(("row", "col"), None, None),
    )
    return jax.shard_map(
        on_device,
        mesh=mesh,
        in_specs=placed,
        out_specs=P(("row", "col"), None, None),
        check_vma=False,
    )
```

```python
import jax
import jax.numpy as jnp
from jax import lax
from jax.experimental import pallas as pl
from jax.experimental.pallas import tpu as pltpu
from jax.sharding import PartitionSpec as P

BLOCK = 64
TAP = 6
TC = 27
LANES = 128
HALF = BLOCK * BLOCK // LANES

highest = lax.Precision.HIGHEST
chunk = 32


def ap_kernel(rows_ref, cols_ref, slots_ref, cnt_ref, a_ref, p_ref, meta_ref, o_ref):
    c = pl.program_id(0)
    capacity = rows_ref.shape[0]
    branches = p_ref.shape[1]

    @pl.when(c == 0)
    def _():
        o_ref[...] = jnp.zeros(o_ref.shape, o_ref.dtype)

    count = cnt_ref[0]

    def body(u, carry):
        t = c * chunk + u

        @pl.when(t < count)
        def _():
            a = a_ref[u]
            col = cols_ref[t]
            row = rows_ref[t]
            for s in range(branches):
                prod = jnp.dot(
                    a, p_ref[col, s], preferred_element_type=jnp.float32, precision=highest
                )
                idx = row * TAP + slots_ref[s * capacity + t]
                o_ref[idx] += prod

        return carry

    lax.fori_loop(0, chunk, body, 0)


def ap_partial(tiles, rows, cols, slots, count, panel, meta, out_rows):
    capacity = tiles.shape[0]
    chunks = capacity // chunk

    def a_map(c, rows_ref, cols_ref, slots_ref, cnt_ref):
        last = (cnt_ref[0] - 1) // chunk
        return (jnp.minimum(c, last), 0, 0)

    grid_spec = pltpu.PrefetchScalarGridSpec(
        num_scalar_prefetch=4,
        grid=(chunks,),
        in_specs=[
            pl.BlockSpec((chunk, BLOCK, BLOCK), a_map),
            pl.BlockSpec(memory_space=pltpu.VMEM),
            pl.BlockSpec(memory_space=pltpu.SMEM),
        ],
        out_specs=pl.BlockSpec(memory_space=pltpu.VMEM),
    )
    return pl.pallas_call(
        ap_kernel,
        out_shape=jax.ShapeDtypeStruct((out_rows * TAP, BLOCK, BLOCK), jnp.float32),
        grid_spec=grid_spec,
        compiler_params=pltpu.CompilerParams(
            dimension_semantics=("arbitrary",), vmem_limit_bytes=56 * 1024 * 1024
        ),
    )(rows, cols, slots, count, tiles, panel, meta)


def on_device(a_vals, a_row, a_col, a_slot, a_count, p_vals, p_owner, p_sub, ap_cslot):
    row_devices = lax.axis_size("row")
    col_devices = lax.axis_size("col")
    capacity = a_vals.shape[2]
    rows_dev = p_vals.shape[0]
    branches = p_vals.shape[1]
    tile_len = p_vals.shape[2]
    group_rows = rows_dev * col_devices
    per_peer = 2
    item_count = rows_dev * branches
    slots_total = row_devices * per_peer

    meta_local = jnp.concatenate(
        [p_owner.reshape(item_count, 1), p_sub.reshape(item_count, 1),
         ap_cslot.reshape(item_count, TAP)], axis=1
    ).astype(jnp.float32)
    meta_all = lax.all_gather(meta_local, "row", axis=0, tiled=False)

    panel = lax.all_gather(p_vals, "row", axis=0, tiled=True)
    panel_tiles = panel.reshape(rows_dev * row_devices, branches, BLOCK, BLOCK)
    partial_value = ap_partial(
        a_vals.reshape(capacity, BLOCK, BLOCK), a_row.reshape(capacity), a_col.reshape(capacity),
        a_slot.reshape(branches * capacity), a_count.reshape(1), panel_tiles,
        meta_all.reshape(row_devices * item_count, TAP + 2), group_rows
    )
    ap_rows = lax.psum_scatter(
        partial_value.reshape(group_rows, TAP, tile_len), "col", scatter_dimension=0, tiled=True
    )

    p4 = p_vals.reshape(rows_dev, branches, BLOCK, BLOCK)
    ap4 = ap_rows.reshape(rows_dev, TAP, BLOCK, BLOCK)
    prods = jnp.einsum("isjk,iqjl->isqkl", p4, ap4, precision=highest)
    prods = prods.reshape(item_count, TAP, tile_len)
    prods = jnp.concatenate([prods, jnp.zeros((1, TAP, tile_len), jnp.float32)], axis=0)

    owners = p_owner.reshape(item_count)
    serial = jnp.arange(item_count, dtype=jnp.int32)
    earlier = (owners[:, None] == owners[None, :]) & (serial[None, :] < serial[:, None])
    placed = owners * per_peer + jnp.sum(earlier.astype(jnp.int32), axis=1)
    slot_ids = jnp.arange(slots_total, dtype=jnp.int32)
    hit = placed[None, :] == slot_ids[:, None]
    source = jnp.where(
        jnp.any(hit, axis=1), jnp.sum(jnp.where(hit, serial[None, :], 0), axis=1), item_count
    )
    outgoing = jnp.take(prods, source, axis=0)
    incoming = lax.all_to_all(outgoing, "row", split_axis=0, concat_axis=0, tiled=True)

    me = lax.axis_index("row").astype(jnp.float32)
    meta_all = meta_all.reshape(row_devices, item_count, TAP + 2)
    match = meta_all[:, :, 0] == me
    rank = jnp.cumsum(match.astype(jnp.int32), axis=1) - 1
    ranks = jnp.arange(per_peer, dtype=jnp.int32)
    pick = match[:, None, :] & (rank[:, None, :] == ranks[None, :, None])
    dest = meta_all[:, :, 1:2] * TC + meta_all[:, :, 2:]
    dest_slot = jnp.sum(jnp.where(pick[..., None], dest[:, None, :, :], 0.0), axis=2)
    valid = jnp.any(pick, axis=2)
    dest_slot = jnp.where(valid[..., None], dest_slot, -1.0).reshape(slots_total * TAP)
    group_coarse = col_devices * TC
    onehot = (
        dest_slot[:, None] == jnp.arange(group_coarse, dtype=jnp.float32)[None, :]
    ).astype(jnp.float32)
    coarse_part = jnp.einsum(
        "ec,ef->cf", onehot, incoming.reshape(slots_total * TAP, tile_len), precision=highest
    )
    coarse = lax.psum_scatter(
        coarse_part.reshape(col_devices, TC, tile_len), "col", scatter_dimension=0, tiled=True
    )
    return coarse


def solution(mesh):
    placed = (
        P("row", "col", None, None),
        P("row", "col", None),
        P("row", "col", None),
        P("row", "col", None, None),
        P("row", "col"),
        P(("row", "col"), None, None),
        P(("row", "col"), None),
        P(("row", "col"), None),
        P(("row", "col"), None, None),
    )
    return jax.shard_map(
        on_device,
        mesh=mesh,
        in_specs=placed,
        out_specs=P(("row", "col"), None, None),
        check_vma=False,
    )
```

```python
import jax
import jax.numpy as jnp
from jax import lax
from jax.experimental import pallas as pl
from jax.experimental.pallas import tpu as pltpu
from jax.sharding import PartitionSpec as P

BLOCK = 64
TAP = 6
TC = 27
LANES = 128
HALF = BLOCK * BLOCK // LANES

highest = lax.Precision.HIGHEST
chunk = 32


def ap_kernel(rows_ref, cols_ref, slots_ref, cnt_ref, a_ref, p_ref, meta_ref, o_ref):
    c = pl.program_id(0)
    capacity = rows_ref.shape[0]
    branches = p_ref.shape[1]

    @pl.when(c == 0)
    def _():
        o_ref[...] = jnp.zeros(o_ref.shape, o_ref.dtype)

    count = cnt_ref[0]

    def body(u, carry):
        t = c * chunk + u
        live = t < count
        a = a_ref[u]
        col = cols_ref[t]
        row = rows_ref[t]
        for s in range(branches):
            prod = jnp.dot(
                a, p_ref[col, s], preferred_element_type=jnp.float32, precision=highest
            )
            idx = row * TAP + slots_ref[s * capacity + t]
            o_ref[idx] += jnp.where(live, prod, 0.0)
        return carry

    @pl.when(c * chunk < count)
    def _():
        lax.fori_loop(0, chunk, body, 0, unroll=True)


def ap_partial(tiles, rows, cols, slots, count, panel, meta, out_rows):
    capacity = tiles.shape[0]
    chunks = capacity // chunk

    def a_map(c, rows_ref, cols_ref, slots_ref, cnt_ref):
        last = (cnt_ref[0] - 1) // chunk
        return (jnp.minimum(c, last), 0, 0)

    grid_spec = pltpu.PrefetchScalarGridSpec(
        num_scalar_prefetch=4,
        grid=(chunks,),
        in_specs=[
            pl.BlockSpec((chunk, BLOCK, BLOCK), a_map),
            pl.BlockSpec(memory_space=pltpu.VMEM),
            pl.BlockSpec(memory_space=pltpu.SMEM),
        ],
        out_specs=pl.BlockSpec(memory_space=pltpu.VMEM),
    )
    return pl.pallas_call(
        ap_kernel,
        out_shape=jax.ShapeDtypeStruct((out_rows * TAP, BLOCK, BLOCK), jnp.float32),
        grid_spec=grid_spec,
        compiler_params=pltpu.CompilerParams(
            dimension_semantics=("arbitrary",), vmem_limit_bytes=56 * 1024 * 1024
        ),
    )(rows, cols, slots, count, tiles, panel, meta)


def on_device(a_vals, a_row, a_col, a_slot, a_count, p_vals, p_owner, p_sub, ap_cslot):
    row_devices = lax.axis_size("row")
    col_devices = lax.axis_size("col")
    capacity = a_vals.shape[2]
    rows_dev = p_vals.shape[0]
    branches = p_vals.shape[1]
    tile_len = p_vals.shape[2]
    group_rows = rows_dev * col_devices
    per_peer = 2
    item_count = rows_dev * branches
    slots_total = row_devices * per_peer

    meta_local = jnp.concatenate(
        [p_owner.reshape(item_count, 1), p_sub.reshape(item_count, 1),
         ap_cslot.reshape(item_count, TAP)], axis=1
    ).astype(jnp.float32)
    meta_all = lax.all_gather(meta_local, "row", axis=0, tiled=False)

    panel = lax.all_gather(p_vals, "row", axis=0, tiled=True)
    panel_tiles = panel.reshape(rows_dev * row_devices, branches, BLOCK, BLOCK)
    partial_value = ap_partial(
        a_vals.reshape(capacity, BLOCK, BLOCK), a_row.reshape(capacity), a_col.reshape(capacity),
        a_slot.reshape(branches * capacity), a_count.reshape(1), panel_tiles,
        meta_all.reshape(row_devices * item_count, TAP + 2), group_rows
    )
    ap_rows = lax.psum_scatter(
        partial_value.reshape(group_rows, TAP, tile_len), "col", scatter_dimension=0, tiled=True
    )

    p4 = p_vals.reshape(rows_dev, branches, BLOCK, BLOCK)
    ap4 = ap_rows.reshape(rows_dev, TAP, BLOCK, BLOCK)
    prods = jnp.einsum("isjk,iqjl->isqkl", p4, ap4, precision=highest)
    prods = prods.reshape(item_count, TAP, tile_len)
    prods = jnp.concatenate([prods, jnp.zeros((1, TAP, tile_len), jnp.float32)], axis=0)

    owners = p_owner.reshape(item_count)
    serial = jnp.arange(item_count, dtype=jnp.int32)
    earlier = (owners[:, None] == owners[None, :]) & (serial[None, :] < serial[:, None])
    placed = owners * per_peer + jnp.sum(earlier.astype(jnp.int32), axis=1)
    slot_ids = jnp.arange(slots_total, dtype=jnp.int32)
    hit = placed[None, :] == slot_ids[:, None]
    source = jnp.where(
        jnp.any(hit, axis=1), jnp.sum(jnp.where(hit, serial[None, :], 0), axis=1), item_count
    )
    outgoing = jnp.take(prods, source, axis=0)
    incoming = lax.all_to_all(outgoing, "row", split_axis=0, concat_axis=0, tiled=True)

    me = lax.axis_index("row").astype(jnp.float32)
    meta_all = meta_all.reshape(row_devices, item_count, TAP + 2)
    match = meta_all[:, :, 0] == me
    rank = jnp.cumsum(match.astype(jnp.int32), axis=1) - 1
    ranks = jnp.arange(per_peer, dtype=jnp.int32)
    pick = match[:, None, :] & (rank[:, None, :] == ranks[None, :, None])
    dest = meta_all[:, :, 1:2] * TC + meta_all[:, :, 2:]
    dest_slot = jnp.sum(jnp.where(pick[..., None], dest[:, None, :, :], 0.0), axis=2)
    valid = jnp.any(pick, axis=2)
    dest_slot = jnp.where(valid[..., None], dest_slot, -1.0).reshape(slots_total * TAP)
    group_coarse = col_devices * TC
    onehot = (
        dest_slot[:, None] == jnp.arange(group_coarse, dtype=jnp.float32)[None, :]
    ).astype(jnp.float32)
    coarse_part = jnp.einsum(
        "ec,ef->cf", onehot, incoming.reshape(slots_total * TAP, tile_len), precision=highest
    )
    coarse = lax.psum_scatter(
        coarse_part.reshape(col_devices, TC, tile_len), "col", scatter_dimension=0, tiled=True
    )
    return coarse


def solution(mesh):
    placed = (
        P("row", "col", None, None),
        P("row", "col", None),
        P("row", "col", None),
        P("row", "col", None, None),
        P("row", "col"),
        P(("row", "col"), None, None),
        P(("row", "col"), None),
        P(("row", "col"), None),
        P(("row", "col"), None, None),
    )
    return jax.shard_map(
        on_device,
        mesh=mesh,
        in_specs=placed,
        out_specs=P(("row", "col"), None, None),
        check_vma=False,
    )
```

```python
import jax
import jax.numpy as jnp
from jax import lax
from jax.experimental import pallas as pl
from jax.experimental.pallas import tpu as pltpu
from jax.sharding import PartitionSpec as P

BLOCK = 64
TAP = 6
TC = 27
LANES = 128
HALF = BLOCK * BLOCK // LANES

highest = lax.Precision.HIGHEST
chunk = 32


def ap_kernel(rows_ref, cols_ref, slots_ref, cnt_ref, a_ref, p2_ref, meta_ref, o_ref, p_scr, acc):
    c = pl.program_id(0)
    capacity = rows_ref.shape[0]
    cols, branches = p2_ref.shape[:2]

    @pl.when(c == 0)
    def _():
        acc[...] = jnp.zeros(acc.shape, acc.dtype)

        def unpack(k, carry):
            col = k // branches
            s = k % branches
            x = p2_ref[col, s]
            even = x[:, :BLOCK]
            odd = pltpu.roll(x, BLOCK, 1)[:, :BLOCK]
            p_scr[col, s] = jnp.concatenate([even, odd], axis=0)
            return carry

        lax.fori_loop(0, cols * branches, unpack, 0, unroll=8)

    count = cnt_ref[0]

    def body(u, carry):
        t = c * chunk + u
        live = t < count
        a = a_ref[u]
        col = cols_ref[t]
        row = rows_ref[t]
        for s in range(branches):
            prod = jnp.dot(
                a, p_scr[col, s], preferred_element_type=jnp.float32, precision=highest
            )
            idx = row * TAP + slots_ref[s * capacity + t]
            acc[idx] += jnp.where(live, prod, 0.0)
        return carry

    @pl.when(c * chunk < count)
    def _():
        lax.fori_loop(0, chunk, body, 0, unroll=True)

    @pl.when(c == pl.num_programs(0) - 1)
    def _():
        def pack(i, carry):
            even = acc[i, pl.ds(0, HALF, stride=2), :]
            odd = acc[i, pl.ds(1, HALF, stride=2), :]
            o_ref[i] = jnp.concatenate([even, odd], axis=1)
            return carry

        lax.fori_loop(0, acc.shape[0], pack, 0, unroll=8)


def ap_partial(tiles, rows, cols, slots, count, panel2, meta, out_rows):
    capacity = tiles.shape[0]
    chunks = capacity // chunk
    ncols, branches = panel2.shape[:2]

    def a_map(c, rows_ref, cols_ref, slots_ref, cnt_ref):
        last = (cnt_ref[0] - 1) // chunk
        return (jnp.minimum(c, last), 0, 0)

    grid_spec = pltpu.PrefetchScalarGridSpec(
        num_scalar_prefetch=4,
        grid=(chunks,),
        in_specs=[
            pl.BlockSpec((chunk, BLOCK, BLOCK), a_map),
            pl.BlockSpec(memory_space=pltpu.VMEM),
            pl.BlockSpec(memory_space=pltpu.SMEM),
        ],
        out_specs=pl.BlockSpec(memory_space=pltpu.VMEM),
        scratch_shapes=[
            pltpu.VMEM((ncols, branches, BLOCK, BLOCK), jnp.float32),
            pltpu.VMEM((out_rows * TAP, BLOCK, BLOCK), jnp.float32),
        ],
    )
    return pl.pallas_call(
        ap_kernel,
        out_shape=jax.ShapeDtypeStruct((out_rows * TAP, HALF, LANES), jnp.float32),
        grid_spec=grid_spec,
        compiler_params=pltpu.CompilerParams(
            dimension_semantics=("arbitrary",), vmem_limit_bytes=60 * 1024 * 1024
        ),
    )(rows, cols, slots, count, tiles, panel2, meta)


def on_device(a_vals, a_row, a_col, a_slot, a_count, p_vals, p_owner, p_sub, ap_cslot):
    row_devices = lax.axis_size("row")
    col_devices = lax.axis_size("col")
    capacity = a_vals.shape[2]
    rows_dev = p_vals.shape[0]
    branches = p_vals.shape[1]
    tile_len = p_vals.shape[2]
    group_rows = rows_dev * col_devices
    per_peer = 2
    item_count = rows_dev * branches
    slots_total = row_devices * per_peer

    meta_local = jnp.concatenate(
        [p_owner.reshape(item_count, 1), p_sub.reshape(item_count, 1),
         ap_cslot.reshape(item_count, TAP)], axis=1
    ).astype(jnp.float32)
    meta_all = lax.all_gather(meta_local, "row", axis=0, tiled=False)

    p2 = p_vals.reshape(rows_dev, branches, HALF, LANES)
    panel2 = lax.all_gather(p2, "row", axis=0, tiled=True)
    a_split = (
        a_vals.reshape(capacity, BLOCK, HALF, 2).transpose(0, 1, 3, 2).reshape(capacity, BLOCK, BLOCK)
    )
    partial_value = ap_partial(
        a_split, a_row.reshape(capacity), a_col.reshape(capacity),
        a_slot.reshape(branches * capacity), a_count.reshape(1), panel2,
        meta_all.reshape(row_devices * item_count, TAP + 2), group_rows
    )
    ap_rows = lax.psum_scatter(
        partial_value.reshape(group_rows, TAP, HALF, LANES), "col", scatter_dimension=0, tiled=True
    )

    owners = p_owner.reshape(item_count)
    serial = jnp.arange(item_count, dtype=jnp.int32)
    earlier = (owners[:, None] == owners[None, :]) & (serial[None, :] < serial[:, None])
    placed = owners * per_peer + jnp.sum(earlier.astype(jnp.int32), axis=1)
    slot_ids = jnp.arange(slots_total, dtype=jnp.int32)
    hit = placed[None, :] == slot_ids[:, None]
    source = jnp.where(
        jnp.any(hit, axis=1), jnp.sum(jnp.where(hit, serial[None, :], 0), axis=1), item_count
    )
    p_items = jnp.concatenate(
        [p_vals.reshape(item_count, BLOCK, BLOCK), jnp.zeros((1, BLOCK, BLOCK), jnp.float32)], axis=0
    )
    left = jnp.take(p_items, source, axis=0)
    right = jnp.take(
        ap_rows.reshape(rows_dev, TAP, BLOCK, BLOCK), jnp.minimum(source // branches, rows_dev - 1),
        axis=0,
    )
    outgoing = jnp.einsum("ejk,eqjl->eqkl", left, right, precision=highest).reshape(
        slots_total, TAP, tile_len
    )
    incoming = lax.all_to_all(outgoing, "row", split_axis=0, concat_axis=0, tiled=True)

    me = lax.axis_index("row").astype(jnp.float32)
    meta_all = meta_all.reshape(row_devices, item_count, TAP + 2)
    match = meta_all[:, :, 0] == me
    rank = jnp.cumsum(match.astype(jnp.int32), axis=1) - 1
    ranks = jnp.arange(per_peer, dtype=jnp.int32)
    pick = match[:, None, :] & (rank[:, None, :] == ranks[None, :, None])
    dest = meta_all[:, :, 1:2] * TC + meta_all[:, :, 2:]
    dest_slot = jnp.sum(jnp.where(pick[..., None], dest[:, None, :, :], 0.0), axis=2)
    valid = jnp.any(pick, axis=2)
    dest_slot = jnp.where(valid[..., None], dest_slot, -1.0).reshape(slots_total * TAP)
    group_coarse = col_devices * TC
    onehot = (
        dest_slot[:, None] == jnp.arange(group_coarse, dtype=jnp.float32)[None, :]
    ).astype(jnp.float32)
    coarse_part = jnp.einsum(
        "ec,ef->cf", onehot, incoming.reshape(slots_total * TAP, tile_len), precision=highest
    )
    coarse = lax.psum_scatter(
        coarse_part.reshape(col_devices, TC, tile_len), "col", scatter_dimension=0, tiled=True
    )
    return coarse


def solution(mesh):
    placed = (
        P("row", "col", None, None),
        P("row", "col", None),
        P("row", "col", None),
        P("row", "col", None, None),
        P("row", "col"),
        P(("row", "col"), None, None),
        P(("row", "col"), None),
        P(("row", "col"), None),
        P(("row", "col"), None, None),
    )
    return jax.shard_map(
        on_device,
        mesh=mesh,
        in_specs=placed,
        out_specs=P(("row", "col"), None, None),
        check_vma=False,
    )
```

```python
import jax
import jax.numpy as jnp
from jax import lax
from jax.experimental import pallas as pl
from jax.experimental.pallas import tpu as pltpu
from jax.sharding import PartitionSpec as P

BLOCK = 64
TAP = 6
TC = 27
LANES = 128
HALF = BLOCK * BLOCK // LANES

highest = lax.Precision.HIGHEST
chunk = 32


def ap_kernel(rows_ref, cols_ref, slots_ref, cnt_ref, a_ref, p2_ref, meta_ref, o_ref, p_scr, acc):
    c = pl.program_id(0)
    capacity = rows_ref.shape[0]
    cols, branches = p2_ref.shape[:2]

    @pl.when(c == 0)
    def _():
        acc[...] = jnp.zeros(acc.shape, acc.dtype)

        def unpack(k, carry):
            col = k // branches
            s = k % branches
            x = p2_ref[col, s]
            even = x[:, :BLOCK]
            odd = pltpu.roll(x, BLOCK, 1)[:, :BLOCK]
            p_scr[col, s] = jnp.concatenate([even, odd], axis=0)
            return carry

        lax.fori_loop(0, cols * branches, unpack, 0, unroll=8)

    count = cnt_ref[0]

    def body(u, carry):
        t = c * chunk + u
        live = t < count
        a = a_ref[u]
        col = cols_ref[t]
        row = rows_ref[t]
        for s in range(branches):
            prod = jnp.dot(
                a, p_scr[col, s], preferred_element_type=jnp.float32, precision=highest
            )
            idx = row * TAP + slots_ref[s * capacity + t]
            acc[idx] += jnp.where(live, prod, 0.0)
        return carry

    @pl.when(c * chunk < count)
    def _():
        lax.fori_loop(0, chunk, body, 0, unroll=True)

    @pl.when(c == pl.num_programs(0) - 1)
    def _():
        def pack(i, carry):
            even = acc[i, pl.ds(0, HALF, stride=2), :]
            odd = acc[i, pl.ds(1, HALF, stride=2), :]
            o_ref[i] = jnp.concatenate([even, odd], axis=1)
            return carry

        lax.fori_loop(0, acc.shape[0], pack, 0, unroll=8)


def ap_partial(tiles, rows, cols, slots, count, panel2, meta, out_rows):
    capacity = tiles.shape[0]
    chunks = capacity // chunk
    ncols, branches = panel2.shape[:2]

    def a_map(c, rows_ref, cols_ref, slots_ref, cnt_ref):
        last = (cnt_ref[0] - 1) // chunk
        return (jnp.minimum(c, last), 0, 0)

    grid_spec = pltpu.PrefetchScalarGridSpec(
        num_scalar_prefetch=4,
        grid=(chunks,),
        in_specs=[
            pl.BlockSpec((chunk, BLOCK, BLOCK), a_map),
            pl.BlockSpec(memory_space=pltpu.VMEM),
            pl.BlockSpec(memory_space=pltpu.SMEM),
        ],
        out_specs=pl.BlockSpec(memory_space=pltpu.VMEM),
        scratch_shapes=[
            pltpu.VMEM((ncols, branches, BLOCK, BLOCK), jnp.float32),
            pltpu.VMEM((out_rows * TAP, BLOCK, BLOCK), jnp.float32),
        ],
    )
    return pl.pallas_call(
        ap_kernel,
        out_shape=jax.ShapeDtypeStruct((out_rows * TAP, HALF, LANES), jnp.float32),
        grid_spec=grid_spec,
        compiler_params=pltpu.CompilerParams(
            dimension_semantics=("arbitrary",), vmem_limit_bytes=60 * 1024 * 1024
        ),
    )(rows, cols, slots, count, tiles, panel2, meta)


def unpack(x):
    return jnp.concatenate([x[:, :BLOCK], pltpu.roll(x, BLOCK, 1)[:, :BLOCK]], axis=0)


def contrib_kernel(src_ref, p2_ref, ap2_ref, o_ref, scr):
    slots = o_ref.shape[0]
    items = p2_ref.shape[0]
    branches = items // ap2_ref.shape[0]

    def body(e, carry):
        item = src_ref[e]
        live = item < items
        it = jnp.minimum(item, items - 1)
        left = unpack(p2_ref[it])
        for q in range(TAP):
            right = unpack(ap2_ref[it // branches, q])
            prod = lax.dot_general(
                left, right, (((0,), (0,)), ((), ())),
                preferred_element_type=jnp.float32, precision=highest,
            )
            scr[...] = jnp.where(live, prod, 0.0)
            even = scr[pl.ds(0, HALF, stride=2), :]
            odd = scr[pl.ds(1, HALF, stride=2), :]
            o_ref[e, q] = jnp.concatenate([even, odd], axis=1)
        return carry

    lax.fori_loop(0, slots, body, 0)


def contributions(source, p2, ap2, slots):
    return pl.pallas_call(
        contrib_kernel,
        out_shape=jax.ShapeDtypeStruct((slots, TAP, HALF, LANES), jnp.float32),
        grid_spec=pltpu.PrefetchScalarGridSpec(
            num_scalar_prefetch=1,
            grid=(1,),
            in_specs=[
                pl.BlockSpec(memory_space=pltpu.VMEM),
                pl.BlockSpec(memory_space=pltpu.VMEM),
            ],
            out_specs=pl.BlockSpec(memory_space=pltpu.VMEM),
            scratch_shapes=[pltpu.VMEM((BLOCK, BLOCK), jnp.float32)],
        ),
    )(source, p2, ap2)


def on_device(a_vals, a_row, a_col, a_slot, a_count, p_vals, p_owner, p_sub, ap_cslot):
    row_devices = lax.axis_size("row")
    col_devices = lax.axis_size("col")
    capacity = a_vals.shape[2]
    rows_dev = p_vals.shape[0]
    branches = p_vals.shape[1]
    tile_len = p_vals.shape[2]
    group_rows = rows_dev * col_devices
    per_peer = 2
    item_count = rows_dev * branches
    slots_total = row_devices * per_peer

    meta_local = jnp.concatenate(
        [p_owner.reshape(item_count, 1), p_sub.reshape(item_count, 1),
         ap_cslot.reshape(item_count, TAP)], axis=1
    ).astype(jnp.float32)
    meta_all = lax.all_gather(meta_local, "row", axis=0, tiled=False)

    p2 = p_vals.reshape(rows_dev, branches, HALF, LANES)
    panel2 = lax.all_gather(p2, "row", axis=0, tiled=True)
    a_split = (
        a_vals.reshape(capacity, BLOCK, HALF, 2).transpose(0, 1, 3, 2).reshape(capacity, BLOCK, BLOCK)
    )
    partial_value = ap_partial(
        a_split, a_row.reshape(capacity), a_col.reshape(capacity),
        a_slot.reshape(branches * capacity), a_count.reshape(1), panel2,
        meta_all.reshape(row_devices * item_count, TAP + 2), group_rows
    )
    ap_rows = lax.psum_scatter(
        partial_value.reshape(group_rows, TAP, HALF, LANES), "col", scatter_dimension=0, tiled=True
    )

    owners = p_owner.reshape(item_count)
    serial = jnp.arange(item_count, dtype=jnp.int32)
    earlier = (owners[:, None] == owners[None, :]) & (serial[None, :] < serial[:, None])
    placed = owners * per_peer + jnp.sum(earlier.astype(jnp.int32), axis=1)
    slot_ids = jnp.arange(slots_total, dtype=jnp.int32)
    hit = placed[None, :] == slot_ids[:, None]
    source = jnp.where(
        jnp.any(hit, axis=1), jnp.sum(jnp.where(hit, serial[None, :], 0), axis=1), item_count
    )
    outgoing = contributions(source, p2.reshape(item_count, HALF, LANES), ap_rows, slots_total)
    incoming = lax.all_to_all(outgoing, "row", split_axis=0, concat_axis=0, tiled=True)

    me = lax.axis_index("row").astype(jnp.float32)
    meta_all = meta_all.reshape(row_devices, item_count, TAP + 2)
    match = meta_all[:, :, 0] == me
    rank = jnp.cumsum(match.astype(jnp.int32), axis=1) - 1
    ranks = jnp.arange(per_peer, dtype=jnp.int32)
    pick = match[:, None, :] & (rank[:, None, :] == ranks[None, :, None])
    dest = meta_all[:, :, 1:2] * TC + meta_all[:, :, 2:]
    dest_slot = jnp.sum(jnp.where(pick[..., None], dest[:, None, :, :], 0.0), axis=2)
    valid = jnp.any(pick, axis=2)
    dest_slot = jnp.where(valid[..., None], dest_slot, -1.0).reshape(slots_total * TAP)
    group_coarse = col_devices * TC
    onehot = (
        dest_slot[:, None] == jnp.arange(group_coarse, dtype=jnp.float32)[None, :]
    ).astype(jnp.float32)
    coarse_part = jnp.einsum("ec,eml->cml", onehot, incoming.reshape(slots_total * TAP, HALF, LANES),
                             precision=highest)
    coarse = lax.psum_scatter(
        coarse_part.reshape(col_devices, TC, HALF, LANES), "col", scatter_dimension=0, tiled=True
    )
    coarse = coarse.reshape(1, TC, tile_len)
    return coarse


def solution(mesh):
    placed = (
        P("row", "col", None, None),
        P("row", "col", None),
        P("row", "col", None),
        P("row", "col", None, None),
        P("row", "col"),
        P(("row", "col"), None, None),
        P(("row", "col"), None),
        P(("row", "col"), None),
        P(("row", "col"), None, None),
    )
    return jax.shard_map(
        on_device,
        mesh=mesh,
        in_specs=placed,
        out_specs=P(("row", "col"), None, None),
        check_vma=False,
    )
```

```python
import jax
import jax.numpy as jnp
from jax import lax
from jax.experimental import pallas as pl
from jax.experimental.pallas import tpu as pltpu
from jax.sharding import PartitionSpec as P

BLOCK = 64
TAP = 6
TC = 27
LANES = 128
RPD = 8
HALF = BLOCK * BLOCK // LANES

highest = lax.Precision.HIGHEST
chunk = 32


def ap_kernel(rows_ref, cols_ref, slots_ref, cnt_ref, a_ref, p2_ref, o_ref, p_scr, acc):
    c = pl.program_id(0)
    capacity = rows_ref.shape[0]
    cols, branches = p_scr.shape[:2]
    per_peer_tiles = p2_ref.shape[0] // (cols // RPD)

    @pl.when(c == 0)
    def _():
        acc[...] = jnp.zeros(acc.shape, acc.dtype)

        def unpack(k, carry):
            col = k // branches
            s = k % branches
            x = p2_ref[(col // RPD) * per_peer_tiles + (col % RPD) * branches + s]
            even = x[:, :BLOCK]
            odd = pltpu.roll(x, BLOCK, 1)[:, :BLOCK]
            p_scr[col, s] = jnp.concatenate([even, odd], axis=0)
            return carry

        lax.fori_loop(0, cols * branches, unpack, 0, unroll=8)

    count = cnt_ref[0]

    def body(u, carry):
        t = c * chunk + u
        live = t < count
        a = a_ref[u]
        col = cols_ref[t]
        row = rows_ref[t]
        for s in range(branches):
            prod = jnp.dot(
                a, p_scr[col, s], preferred_element_type=jnp.float32, precision=highest
            )
            idx = row * TAP + slots_ref[s * capacity + t]
            acc[idx] += jnp.where(live, prod, 0.0)
        return carry

    @pl.when(c * chunk < count)
    def _():
        lax.fori_loop(0, chunk, body, 0, unroll=True)

    @pl.when(c == pl.num_programs(0) - 1)
    def _():
        def pack(i, carry):
            even = acc[i, pl.ds(0, HALF, stride=2), :]
            odd = acc[i, pl.ds(1, HALF, stride=2), :]
            o_ref[i] = jnp.concatenate([even, odd], axis=1)
            return carry

        lax.fori_loop(0, acc.shape[0], pack, 0, unroll=8)


def ap_partial(tiles, rows, cols, slots, count, panel2, ncols, branches, out_rows):
    capacity = tiles.shape[0]
    chunks = capacity // chunk

    def a_map(c, rows_ref, cols_ref, slots_ref, cnt_ref):
        last = (cnt_ref[0] - 1) // chunk
        return (jnp.minimum(c, last), 0, 0)

    grid_spec = pltpu.PrefetchScalarGridSpec(
        num_scalar_prefetch=4,
        grid=(chunks,),
        in_specs=[
            pl.BlockSpec((chunk, BLOCK, BLOCK), a_map),
            pl.BlockSpec(memory_space=pltpu.VMEM),
        ],
        out_specs=pl.BlockSpec(memory_space=pltpu.VMEM),
        scratch_shapes=[
            pltpu.VMEM((ncols, branches, BLOCK, BLOCK), jnp.float32),
            pltpu.VMEM((out_rows * TAP, BLOCK, BLOCK), jnp.float32),
        ],
    )
    return pl.pallas_call(
        ap_kernel,
        out_shape=jax.ShapeDtypeStruct((out_rows * TAP, HALF, LANES), jnp.float32),
        grid_spec=grid_spec,
        compiler_params=pltpu.CompilerParams(
            dimension_semantics=("arbitrary",), vmem_limit_bytes=60 * 1024 * 1024
        ),
    )(rows, cols, slots, count, tiles, panel2)


def unpack(x):
    return jnp.concatenate([x[:, :BLOCK], pltpu.roll(x, BLOCK, 1)[:, :BLOCK]], axis=0)


def contrib_kernel(src_ref, p2_ref, ap2_ref, o_ref, scr):
    slots = o_ref.shape[0]
    items = p2_ref.shape[0]
    branches = items // ap2_ref.shape[0]

    def body(e, carry):
        item = src_ref[e]
        live = item < items
        it = jnp.minimum(item, items - 1)
        left = unpack(p2_ref[it]).T
        for q in range(TAP):
            right = unpack(ap2_ref[it // branches, q])
            prod = jnp.dot(left, right, preferred_element_type=jnp.float32, precision=highest)
            scr[...] = jnp.where(live, prod, 0.0)
            even = scr[pl.ds(0, HALF, stride=2), :]
            odd = scr[pl.ds(1, HALF, stride=2), :]
            o_ref[e, q] = jnp.concatenate([even, odd], axis=1)
        return carry

    lax.fori_loop(0, slots, body, 0)


def contributions(source, p2, ap2, slots):
    return pl.pallas_call(
        contrib_kernel,
        out_shape=jax.ShapeDtypeStruct((slots, TAP, HALF, LANES), jnp.float32),
        grid_spec=pltpu.PrefetchScalarGridSpec(
            num_scalar_prefetch=1,
            grid=(1,),
            in_specs=[
                pl.BlockSpec(memory_space=pltpu.VMEM),
                pl.BlockSpec(memory_space=pltpu.VMEM),
            ],
            out_specs=pl.BlockSpec(memory_space=pltpu.VMEM),
            scratch_shapes=[pltpu.VMEM((BLOCK, BLOCK), jnp.float32)],
        ),
    )(source, p2, ap2)


def on_device(a_vals, a_row, a_col, a_slot, a_count, p_vals, p_owner, p_sub, ap_cslot):
    row_devices = lax.axis_size("row")
    col_devices = lax.axis_size("col")
    capacity = a_vals.shape[2]
    rows_dev = p_vals.shape[0]
    branches = p_vals.shape[1]
    tile_len = p_vals.shape[2]
    group_rows = rows_dev * col_devices
    per_peer = 2
    item_count = rows_dev * branches
    slots_total = row_devices * per_peer

    meta_local = jnp.concatenate(
        [p_owner.reshape(item_count, 1), p_sub.reshape(item_count, 1),
         ap_cslot.reshape(item_count, TAP)], axis=1
    ).astype(jnp.float32)
    meta_tile = jnp.pad(meta_local.reshape(-1), (0, tile_len - item_count * (TAP + 2)))
    p2 = p_vals.reshape(item_count, HALF, LANES)
    sent = jnp.concatenate([p2, meta_tile.reshape(1, HALF, LANES)], axis=0)
    panel2 = lax.all_gather(sent, "row", axis=0, tiled=True)
    meta_all = panel2.reshape(row_devices, item_count + 1, tile_len)[:, item_count, :item_count * (TAP + 2)]
    a_split = (
        a_vals.reshape(capacity, BLOCK, HALF, 2).transpose(0, 1, 3, 2).reshape(capacity, BLOCK, BLOCK)
    )
    partial_value = ap_partial(
        a_split, a_row.reshape(capacity), a_col.reshape(capacity),
        a_slot.reshape(branches * capacity), a_count.reshape(1), panel2,
        rows_dev * row_devices, branches, group_rows
    )
    ap_rows = lax.psum_scatter(
        partial_value.reshape(group_rows, TAP, HALF, LANES), "col", scatter_dimension=0, tiled=True
    )

    owners = p_owner.reshape(item_count)
    serial = jnp.arange(item_count, dtype=jnp.int32)
    earlier = (owners[:, None] == owners[None, :]) & (serial[None, :] < serial[:, None])
    placed = owners * per_peer + jnp.sum(earlier.astype(jnp.int32), axis=1)
    slot_ids = jnp.arange(slots_total, dtype=jnp.int32)
    hit = placed[None, :] == slot_ids[:, None]
    source = jnp.where(
        jnp.any(hit, axis=1), jnp.sum(jnp.where(hit, serial[None, :], 0), axis=1), item_count
    )
    outgoing = contributions(source, p2, ap_rows, slots_total)
    incoming = lax.all_to_all(outgoing, "row", split_axis=0, concat_axis=0, tiled=True)

    me = lax.axis_index("row").astype(jnp.float32)
    meta_all = meta_all.reshape(row_devices, item_count, TAP + 2)
    match = meta_all[:, :, 0] == me
    rank = jnp.cumsum(match.astype(jnp.int32), axis=1) - 1
    ranks = jnp.arange(per_peer, dtype=jnp.int32)
    pick = match[:, None, :] & (rank[:, None, :] == ranks[None, :, None])
    dest = meta_all[:, :, 1:2] * TC + meta_all[:, :, 2:]
    dest_slot = jnp.sum(jnp.where(pick[..., None], dest[:, None, :, :], 0.0), axis=2)
    valid = jnp.any(pick, axis=2)
    dest_slot = jnp.where(valid[..., None], dest_slot, -1.0).reshape(slots_total * TAP)
    group_coarse = col_devices * TC
    onehot = (
        dest_slot[:, None] == jnp.arange(group_coarse, dtype=jnp.float32)[None, :]
    ).astype(jnp.float32)
    coarse_part = jnp.einsum("ec,eml->cml", onehot, incoming.reshape(slots_total * TAP, HALF, LANES),
                             precision=highest)
    coarse = lax.psum_scatter(
        coarse_part.reshape(col_devices, TC, HALF, LANES), "col", scatter_dimension=0, tiled=True
    )
    coarse = coarse.reshape(1, TC, tile_len)
    return coarse


def solution(mesh):
    placed = (
        P("row", "col", None, None),
        P("row", "col", None),
        P("row", "col", None),
        P("row", "col", None, None),
        P("row", "col"),
        P(("row", "col"), None, None),
        P(("row", "col"), None),
        P(("row", "col"), None),
        P(("row", "col"), None, None),
    )
    return jax.shard_map(
        on_device,
        mesh=mesh,
        in_specs=placed,
        out_specs=P(("row", "col"), None, None),
        check_vma=False,
    )
```

```python
import jax
import jax.numpy as jnp
from jax import lax
from jax.experimental import pallas as pl
from jax.experimental.pallas import tpu as pltpu
from jax.sharding import PartitionSpec as P

BLOCK = 64
TAP = 6
TC = 27
LANES = 128
RPD = 8
HALF = BLOCK * BLOCK // LANES

highest = lax.Precision.HIGHEST
chunk = 32


def ap_kernel(rows_ref, cols_ref, slots_ref, cnt_ref, a_ref, p2_ref, o_ref, p_scr, acc):
    c = pl.program_id(0)
    capacity = rows_ref.shape[0]
    cols, branches = p_scr.shape[:2]
    per_peer_tiles = p2_ref.shape[0] // (cols // RPD)

    @pl.when(c == 0)
    def _():
        acc[...] = jnp.zeros(acc.shape, acc.dtype)

        def unpack(k, carry):
            col = k // branches
            s = k % branches
            x = p2_ref[(col // RPD) * per_peer_tiles + (col % RPD) * branches + s]
            even = x[:, :BLOCK]
            odd = pltpu.roll(x, BLOCK, 1)[:, :BLOCK]
            p_scr[col, s] = jnp.concatenate([even, odd], axis=0)
            return carry

        lax.fori_loop(0, cols * branches, unpack, 0, unroll=8)

    count = cnt_ref[0]

    def body(u, carry):
        t = c * chunk + u
        live = t < count
        a = a_ref[u]
        col = cols_ref[t]
        row = rows_ref[t]
        for s in range(branches):
            prod = jnp.dot(
                a, p_scr[col, s], preferred_element_type=jnp.float32, precision=highest
            )
            idx = row * TAP + slots_ref[s * capacity + t]
            acc[idx] += jnp.where(live, prod, 0.0)
        return carry

    @pl.when(c * chunk < count)
    def _():
        lax.fori_loop(0, chunk, body, 0, unroll=True)

    @pl.when(c == pl.num_programs(0) - 1)
    def _():
        def pack(i, carry):
            even = acc[i, pl.ds(0, HALF, stride=2), :]
            odd = acc[i, pl.ds(1, HALF, stride=2), :]
            o_ref[i] = jnp.concatenate([even, odd], axis=1)
            return carry

        lax.fori_loop(0, acc.shape[0], pack, 0, unroll=8)


def ap_partial(tiles, rows, cols, slots, count, panel2, ncols, branches, out_rows):
    capacity = tiles.shape[0]
    chunks = capacity // chunk

    def a_map(c, rows_ref, cols_ref, slots_ref, cnt_ref):
        last = (cnt_ref[0] - 1) // chunk
        return (jnp.minimum(c, last), 0, 0)

    grid_spec = pltpu.PrefetchScalarGridSpec(
        num_scalar_prefetch=4,
        grid=(chunks,),
        in_specs=[
            pl.BlockSpec((chunk, BLOCK, BLOCK), a_map),
            pl.BlockSpec(memory_space=pltpu.VMEM),
        ],
        out_specs=pl.BlockSpec(memory_space=pltpu.VMEM),
        scratch_shapes=[
            pltpu.VMEM((ncols, branches, BLOCK, BLOCK), jnp.float32),
            pltpu.VMEM((out_rows * TAP, BLOCK, BLOCK), jnp.float32),
        ],
    )
    return pl.pallas_call(
        ap_kernel,
        out_shape=jax.ShapeDtypeStruct((out_rows * TAP, HALF, LANES), jnp.float32),
        grid_spec=grid_spec,
        compiler_params=pltpu.CompilerParams(
            dimension_semantics=("arbitrary",), vmem_limit_bytes=60 * 1024 * 1024
        ),
    )(rows, cols, slots, count, tiles, panel2)


def unpack(x):
    return jnp.concatenate([x[:, :BLOCK], pltpu.roll(x, BLOCK, 1)[:, :BLOCK]], axis=0)


def contrib_kernel(src_ref, p2_ref, ap2_ref, o_ref, scr):
    slots = o_ref.shape[0]
    items = p2_ref.shape[0]
    branches = items // ap2_ref.shape[0]

    def body(e, carry):
        item = src_ref[e]

        @pl.when(item < items)
        def _():
            left = unpack(p2_ref[item]).T
            for q in range(TAP):
                right = unpack(ap2_ref[item // branches, q])
                scr[...] = jnp.dot(left, right, preferred_element_type=jnp.float32, precision=highest)
                even = scr[pl.ds(0, HALF, stride=2), :]
                odd = scr[pl.ds(1, HALF, stride=2), :]
                o_ref[e, q] = jnp.concatenate([even, odd], axis=1)

        @pl.when(item >= items)
        def _():
            o_ref[e] = jnp.zeros(o_ref.shape[1:], o_ref.dtype)

        return carry

    lax.fori_loop(0, slots, body, 0)


def contributions(source, p2, ap2, slots):
    return pl.pallas_call(
        contrib_kernel,
        out_shape=jax.ShapeDtypeStruct((slots, TAP, HALF, LANES), jnp.float32),
        grid_spec=pltpu.PrefetchScalarGridSpec(
            num_scalar_prefetch=1,
            grid=(1,),
            in_specs=[
                pl.BlockSpec(memory_space=pltpu.VMEM),
                pl.BlockSpec(memory_space=pltpu.VMEM),
            ],
            out_specs=pl.BlockSpec(memory_space=pltpu.VMEM),
            scratch_shapes=[pltpu.VMEM((BLOCK, BLOCK), jnp.float32)],
        ),
    )(source, p2, ap2)


def on_device(a_vals, a_row, a_col, a_slot, a_count, p_vals, p_owner, p_sub, ap_cslot):
    row_devices = lax.axis_size("row")
    col_devices = lax.axis_size("col")
    capacity = a_vals.shape[2]
    rows_dev = p_vals.shape[0]
    branches = p_vals.shape[1]
    tile_len = p_vals.shape[2]
    group_rows = rows_dev * col_devices
    per_peer = 2
    item_count = rows_dev * branches
    slots_total = row_devices * per_peer

    meta_local = jnp.concatenate(
        [p_owner.reshape(item_count, 1), p_sub.reshape(item_count, 1),
         ap_cslot.reshape(item_count, TAP)], axis=1
    ).astype(jnp.float32)
    meta_tile = jnp.pad(meta_local.reshape(-1), (0, tile_len - item_count * (TAP + 2)))
    p2 = p_vals.reshape(item_count, HALF, LANES)
    sent = jnp.concatenate([p2, meta_tile.reshape(1, HALF, LANES)], axis=0)
    panel2 = lax.all_gather(sent, "row", axis=0, tiled=True)
    meta_all = panel2.reshape(row_devices, item_count + 1, tile_len)[:, item_count, :item_count * (TAP + 2)]
    a_split = (
        a_vals.reshape(capacity, BLOCK, HALF, 2).transpose(0, 1, 3, 2).reshape(capacity, BLOCK, BLOCK)
    )
    partial_value = ap_partial(
        a_split, a_row.reshape(capacity), a_col.reshape(capacity),
        a_slot.reshape(branches * capacity), a_count.reshape(1), panel2,
        rows_dev * row_devices, branches, group_rows
    )
    ap_rows = lax.psum_scatter(
        partial_value.reshape(group_rows, TAP, HALF, LANES), "col", scatter_dimension=0, tiled=True
    )

    owners = p_owner.reshape(item_count)
    serial = jnp.arange(item_count, dtype=jnp.int32)
    earlier = (owners[:, None] == owners[None, :]) & (serial[None, :] < serial[:, None])
    placed = owners * per_peer + jnp.sum(earlier.astype(jnp.int32), axis=1)
    slot_ids = jnp.arange(slots_total, dtype=jnp.int32)
    hit = placed[None, :] == slot_ids[:, None]
    source = jnp.where(
        jnp.any(hit, axis=1), jnp.sum(jnp.where(hit, serial[None, :], 0), axis=1), item_count
    )
    by_rank = source.reshape(row_devices, per_peer)
    incoming = []
    for k in range(per_peer):
        outgoing = contributions(by_rank[:, k], p2, ap_rows, row_devices)
        incoming.append(lax.all_to_all(outgoing, "row", split_axis=0, concat_axis=0, tiled=True))
    incoming = jnp.stack(incoming, axis=1)

    me = lax.axis_index("row").astype(jnp.float32)
    meta_all = meta_all.reshape(row_devices, item_count, TAP + 2)
    match = meta_all[:, :, 0] == me
    rank = jnp.cumsum(match.astype(jnp.int32), axis=1) - 1
    ranks = jnp.arange(per_peer, dtype=jnp.int32)
    pick = match[:, None, :] & (rank[:, None, :] == ranks[None, :, None])
    dest = meta_all[:, :, 1:2] * TC + meta_all[:, :, 2:]
    dest_slot = jnp.sum(jnp.where(pick[..., None], dest[:, None, :, :], 0.0), axis=2)
    valid = jnp.any(pick, axis=2)
    dest_slot = jnp.where(valid[..., None], dest_slot, -1.0).reshape(slots_total * TAP)
    group_coarse = col_devices * TC
    onehot = (
        dest_slot[:, None] == jnp.arange(group_coarse, dtype=jnp.float32)[None, :]
    ).astype(jnp.float32)
    coarse_part = jnp.einsum("ec,eml->cml", onehot, incoming.reshape(slots_total * TAP, HALF, LANES),
                             precision=highest)
    coarse = lax.psum_scatter(
        coarse_part.reshape(col_devices, TC, HALF, LANES), "col", scatter_dimension=0, tiled=True
    )
    coarse = coarse.reshape(1, TC, tile_len)
    return coarse


def solution(mesh):
    placed = (
        P("row", "col", None, None),
        P("row", "col", None),
        P("row", "col", None),
        P("row", "col", None, None),
        P("row", "col"),
        P(("row", "col"), None, None),
        P(("row", "col"), None),
        P(("row", "col"), None),
        P(("row", "col"), None, None),
    )
    return jax.shard_map(
        on_device,
        mesh=mesh,
        in_specs=placed,
        out_specs=P(("row", "col"), None, None),
        check_vma=False,
    )
```

```python
import jax
import jax.numpy as jnp
from jax import lax
from jax.experimental import pallas as pl
from jax.experimental.pallas import tpu as pltpu
from jax.sharding import PartitionSpec as P

BLOCK = 64
TAP = 6
TC = 27
LANES = 128
RPD = 8
HALF = BLOCK * BLOCK // LANES

highest = lax.Precision.HIGHEST
chunk = 32


def ap_kernel(rows_ref, cols_ref, slots_ref, cnt_ref, a_ref, p2_ref, o_ref, p_scr, acc):
    c = pl.program_id(0)
    capacity = rows_ref.shape[0]
    cols, branches = p_scr.shape[:2]
    per_peer_tiles = p2_ref.shape[0] // (cols // RPD)

    @pl.when(c == 0)
    def _():
        acc[...] = jnp.zeros(acc.shape, acc.dtype)

        def unpack(k, carry):
            col = k // branches
            s = k % branches
            x = p2_ref[(col // RPD) * per_peer_tiles + (col % RPD) * branches + s]
            even = x[:, :BLOCK]
            odd = pltpu.roll(x, BLOCK, 1)[:, :BLOCK]
            p_scr[col, s] = jnp.concatenate([even, odd], axis=0)
            return carry

        lax.fori_loop(0, cols * branches, unpack, 0, unroll=8)

    count = cnt_ref[0]

    def body(u, carry):
        t = c * chunk + u
        live = t < count
        a = a_ref[u]
        col = cols_ref[t]
        row = rows_ref[t]
        for s in range(branches):
            prod = jnp.dot(
                a, p_scr[col, s], preferred_element_type=jnp.float32, precision=lax.Precision.HIGH
            )
            idx = row * TAP + slots_ref[s * capacity + t]
            acc[idx] += jnp.where(live, prod, 0.0)
        return carry

    @pl.when(c * chunk < count)
    def _():
        lax.fori_loop(0, chunk, body, 0, unroll=True)

    @pl.when(c == pl.num_programs(0) - 1)
    def _():
        def pack(i, carry):
            even = acc[i, pl.ds(0, HALF, stride=2), :]
            odd = acc[i, pl.ds(1, HALF, stride=2), :]
            o_ref[i] = jnp.concatenate([even, odd], axis=1)
            return carry

        lax.fori_loop(0, acc.shape[0], pack, 0, unroll=8)


def ap_partial(tiles, rows, cols, slots, count, panel2, ncols, branches, out_rows):
    capacity = tiles.shape[0]
    chunks = capacity // chunk

    def a_map(c, rows_ref, cols_ref, slots_ref, cnt_ref):
        last = (cnt_ref[0] - 1) // chunk
        return (jnp.minimum(c, last), 0, 0)

    grid_spec = pltpu.PrefetchScalarGridSpec(
        num_scalar_prefetch=4,
        grid=(chunks,),
        in_specs=[
            pl.BlockSpec((chunk, BLOCK, BLOCK), a_map),
            pl.BlockSpec(memory_space=pltpu.VMEM),
        ],
        out_specs=pl.BlockSpec(memory_space=pltpu.VMEM),
        scratch_shapes=[
            pltpu.VMEM((ncols, branches, BLOCK, BLOCK), jnp.float32),
            pltpu.VMEM((out_rows * TAP, BLOCK, BLOCK), jnp.float32),
        ],
    )
    return pl.pallas_call(
        ap_kernel,
        out_shape=jax.ShapeDtypeStruct((out_rows * TAP, HALF, LANES), jnp.float32),
        grid_spec=grid_spec,
        compiler_params=pltpu.CompilerParams(
            dimension_semantics=("arbitrary",), vmem_limit_bytes=60 * 1024 * 1024
        ),
    )(rows, cols, slots, count, tiles, panel2)


def unpack(x):
    return jnp.concatenate([x[:, :BLOCK], pltpu.roll(x, BLOCK, 1)[:, :BLOCK]], axis=0)


def contrib_kernel(src_ref, p2_ref, ap2_ref, o_ref, scr):
    slots = o_ref.shape[0]
    items = p2_ref.shape[0]
    branches = items // ap2_ref.shape[0]

    def body(e, carry):
        item = src_ref[e]

        @pl.when(item < items)
        def _():
            left = unpack(p2_ref[item]).T
            for q in range(TAP):
                right = unpack(ap2_ref[item // branches, q])
                scr[...] = jnp.dot(left, right, preferred_element_type=jnp.float32, precision=highest)
                even = scr[pl.ds(0, HALF, stride=2), :]
                odd = scr[pl.ds(1, HALF, stride=2), :]
                o_ref[e, q] = jnp.concatenate([even, odd], axis=1)

        @pl.when(item >= items)
        def _():
            o_ref[e] = jnp.zeros(o_ref.shape[1:], o_ref.dtype)

        return carry

    lax.fori_loop(0, slots, body, 0)


def contributions(source, p2, ap2, slots):
    return pl.pallas_call(
        contrib_kernel,
        out_shape=jax.ShapeDtypeStruct((slots, TAP, HALF, LANES), jnp.float32),
        grid_spec=pltpu.PrefetchScalarGridSpec(
            num_scalar_prefetch=1,
            grid=(1,),
            in_specs=[
                pl.BlockSpec(memory_space=pltpu.VMEM),
                pl.BlockSpec(memory_space=pltpu.VMEM),
            ],
            out_specs=pl.BlockSpec(memory_space=pltpu.VMEM),
            scratch_shapes=[pltpu.VMEM((BLOCK, BLOCK), jnp.float32)],
        ),
    )(source, p2, ap2)


def on_device(a_vals, a_row, a_col, a_slot, a_count, p_vals, p_owner, p_sub, ap_cslot):
    row_devices = lax.axis_size("row")
    col_devices = lax.axis_size("col")
    capacity = a_vals.shape[2]
    rows_dev = p_vals.shape[0]
    branches = p_vals.shape[1]
    tile_len = p_vals.shape[2]
    group_rows = rows_dev * col_devices
    per_peer = 2
    item_count = rows_dev * branches
    slots_total = row_devices * per_peer

    meta_local = jnp.concatenate(
        [p_owner.reshape(item_count, 1), p_sub.reshape(item_count, 1),
         ap_cslot.reshape(item_count, TAP)], axis=1
    ).astype(jnp.float32)
    meta_tile = jnp.pad(meta_local.reshape(-1), (0, tile_len - item_count * (TAP + 2)))
    p2 = p_vals.reshape(item_count, HALF, LANES)
    sent = jnp.concatenate([p2, meta_tile.reshape(1, HALF, LANES)], axis=0)
    panel2 = lax.all_gather(sent, "row", axis=0, tiled=True)
    meta_all = panel2.reshape(row_devices, item_count + 1, tile_len)[:, item_count, :item_count * (TAP + 2)]
    a_split = (
        a_vals.reshape(capacity, BLOCK, HALF, 2).transpose(0, 1, 3, 2).reshape(capacity, BLOCK, BLOCK)
    )
    partial_value = ap_partial(
        a_split, a_row.reshape(capacity), a_col.reshape(capacity),
        a_slot.reshape(branches * capacity), a_count.reshape(1), panel2,
        rows_dev * row_devices, branches, group_rows
    )
    ap_rows = lax.psum_scatter(
        partial_value.reshape(group_rows, TAP, HALF, LANES), "col", scatter_dimension=0, tiled=True
    )

    owners = p_owner.reshape(item_count)
    serial = jnp.arange(item_count, dtype=jnp.int32)
    earlier = (owners[:, None] == owners[None, :]) & (serial[None, :] < serial[:, None])
    placed = owners * per_peer + jnp.sum(earlier.astype(jnp.int32), axis=1)
    slot_ids = jnp.arange(slots_total, dtype=jnp.int32)
    hit = placed[None, :] == slot_ids[:, None]
    source = jnp.where(
        jnp.any(hit, axis=1), jnp.sum(jnp.where(hit, serial[None, :], 0), axis=1), item_count
    )
    by_rank = source.reshape(row_devices, per_peer)
    incoming = []
    for k in range(per_peer):
        outgoing = contributions(by_rank[:, k], p2, ap_rows, row_devices)
        incoming.append(lax.all_to_all(outgoing, "row", split_axis=0, concat_axis=0, tiled=True))
    incoming = jnp.stack(incoming, axis=1)

    me = lax.axis_index("row").astype(jnp.float32)
    meta_all = meta_all.reshape(row_devices, item_count, TAP + 2)
    match = meta_all[:, :, 0] == me
    rank = jnp.cumsum(match.astype(jnp.int32), axis=1) - 1
    ranks = jnp.arange(per_peer, dtype=jnp.int32)
    pick = match[:, None, :] & (rank[:, None, :] == ranks[None, :, None])
    dest = meta_all[:, :, 1:2] * TC + meta_all[:, :, 2:]
    dest_slot = jnp.sum(jnp.where(pick[..., None], dest[:, None, :, :], 0.0), axis=2)
    valid = jnp.any(pick, axis=2)
    dest_slot = jnp.where(valid[..., None], dest_slot, -1.0).reshape(slots_total * TAP)
    group_coarse = col_devices * TC
    onehot = (
        dest_slot[:, None] == jnp.arange(group_coarse, dtype=jnp.float32)[None, :]
    ).astype(jnp.float32)
    coarse_part = jnp.einsum("ec,eml->cml", onehot, incoming.reshape(slots_total * TAP, HALF, LANES),
                             precision=highest)
    coarse = lax.psum_scatter(
        coarse_part.reshape(col_devices, TC, HALF, LANES), "col", scatter_dimension=0, tiled=True
    )
    coarse = coarse.reshape(1, TC, tile_len)
    return coarse


def solution(mesh):
    placed = (
        P("row", "col", None, None),
        P("row", "col", None),
        P("row", "col", None),
        P("row", "col", None, None),
        P("row", "col"),
        P(("row", "col"), None, None),
        P(("row", "col"), None),
        P(("row", "col"), None),
        P(("row", "col"), None, None),
    )
    return jax.shard_map(
        on_device,
        mesh=mesh,
        in_specs=placed,
        out_specs=P(("row", "col"), None, None),
        check_vma=False,
    )
```

```python
import jax
import jax.numpy as jnp
from jax import lax
from jax.experimental import pallas as pl
from jax.experimental.pallas import tpu as pltpu
from jax.sharding import PartitionSpec as P

BLOCK = 64
TAP = 6
TC = 27
LANES = 128
RPD = 8
HALF = BLOCK * BLOCK // LANES

highest = lax.Precision.HIGHEST
chunk = 64


def ap_kernel(rows_ref, cols_ref, slots_ref, cnt_ref, a_ref, p2_ref, o_ref, p_scr, acc):
    c = pl.program_id(0)
    capacity = rows_ref.shape[0]
    cols, branches = p_scr.shape[:2]
    per_peer_tiles = p2_ref.shape[0] // (cols // RPD)

    @pl.when(c == 0)
    def _():
        acc[...] = jnp.zeros(acc.shape, acc.dtype)

        def unpack(k, carry):
            col = k // branches
            s = k % branches
            x = p2_ref[(col // RPD) * per_peer_tiles + (col % RPD) * branches + s]
            even = x[:, :BLOCK]
            odd = pltpu.roll(x, BLOCK, 1)[:, :BLOCK]
            p_scr[col, s] = jnp.concatenate([even, odd], axis=0)
            return carry

        lax.fori_loop(0, cols * branches, unpack, 0, unroll=8)

    count = cnt_ref[0]

    def body(u, carry):
        t = c * chunk + u
        live = t < count
        a = a_ref[u]
        col = cols_ref[t]
        row = rows_ref[t]
        for s in range(branches):
            prod = jnp.dot(
                a, p_scr[col, s], preferred_element_type=jnp.float32, precision=lax.Precision.HIGH
            )
            idx = row * TAP + slots_ref[s * capacity + t]
            acc[idx] += jnp.where(live, prod, 0.0)
        return carry

    @pl.when(c * chunk < count)
    def _():
        lax.fori_loop(0, chunk, body, 0, unroll=True)

    @pl.when(c == pl.num_programs(0) - 1)
    def _():
        def pack(i, carry):
            even = acc[i, pl.ds(0, HALF, stride=2), :]
            odd = acc[i, pl.ds(1, HALF, stride=2), :]
            o_ref[i] = jnp.concatenate([even, odd], axis=1)
            return carry

        lax.fori_loop(0, acc.shape[0], pack, 0, unroll=8)


def ap_partial(tiles, rows, cols, slots, count, panel2, ncols, branches, out_rows):
    capacity = tiles.shape[0]
    chunks = capacity // chunk

    def a_map(c, rows_ref, cols_ref, slots_ref, cnt_ref):
        last = (cnt_ref[0] - 1) // chunk
        return (jnp.minimum(c, last), 0, 0)

    grid_spec = pltpu.PrefetchScalarGridSpec(
        num_scalar_prefetch=4,
        grid=(chunks,),
        in_specs=[
            pl.BlockSpec((chunk, BLOCK, BLOCK), a_map),
            pl.BlockSpec(memory_space=pltpu.VMEM),
        ],
        out_specs=pl.BlockSpec(memory_space=pltpu.VMEM),
        scratch_shapes=[
            pltpu.VMEM((ncols, branches, BLOCK, BLOCK), jnp.float32),
            pltpu.VMEM((out_rows * TAP, BLOCK, BLOCK), jnp.float32),
        ],
    )
    return pl.pallas_call(
        ap_kernel,
        out_shape=jax.ShapeDtypeStruct((out_rows * TAP, HALF, LANES), jnp.float32),
        grid_spec=grid_spec,
        compiler_params=pltpu.CompilerParams(
            dimension_semantics=("arbitrary",), vmem_limit_bytes=60 * 1024 * 1024
        ),
    )(rows, cols, slots, count, tiles, panel2)


def unpack(x):
    return jnp.concatenate([x[:, :BLOCK], pltpu.roll(x, BLOCK, 1)[:, :BLOCK]], axis=0)


def contrib_kernel(src_ref, p2_ref, ap2_ref, o_ref, scr):
    slots = o_ref.shape[0]
    items = p2_ref.shape[0]
    branches = items // ap2_ref.shape[0]

    def body(e, carry):
        item = src_ref[e]

        @pl.when(item < items)
        def _():
            left = unpack(p2_ref[item]).T
            for q in range(TAP):
                right = unpack(ap2_ref[item // branches, q])
                scr[...] = jnp.dot(
                    left, right, preferred_element_type=jnp.float32, precision=lax.Precision.HIGH
                )
                even = scr[pl.ds(0, HALF, stride=2), :]
                odd = scr[pl.ds(1, HALF, stride=2), :]
                o_ref[e, q] = jnp.concatenate([even, odd], axis=1)

        @pl.when(item >= items)
        def _():
            o_ref[e] = jnp.zeros(o_ref.shape[1:], o_ref.dtype)

        return carry

    lax.fori_loop(0, slots, body, 0)


def contributions(source, p2, ap2, slots):
    return pl.pallas_call(
        contrib_kernel,
        out_shape=jax.ShapeDtypeStruct((slots, TAP, HALF, LANES), jnp.float32),
        grid_spec=pltpu.PrefetchScalarGridSpec(
            num_scalar_prefetch=1,
            grid=(1,),
            in_specs=[
                pl.BlockSpec(memory_space=pltpu.VMEM),
                pl.BlockSpec(memory_space=pltpu.VMEM),
            ],
            out_specs=pl.BlockSpec(memory_space=pltpu.VMEM),
            scratch_shapes=[pltpu.VMEM((BLOCK, BLOCK), jnp.float32)],
        ),
    )(source, p2, ap2)


def on_device(a_vals, a_row, a_col, a_slot, a_count, p_vals, p_owner, p_sub, ap_cslot):
    row_devices = lax.axis_size("row")
    col_devices = lax.axis_size("col")
    capacity = a_vals.shape[2]
    rows_dev = p_vals.shape[0]
    branches = p_vals.shape[1]
    tile_len = p_vals.shape[2]
    group_rows = rows_dev * col_devices
    per_peer = 2
    item_count = rows_dev * branches
    slots_total = row_devices * per_peer

    meta_local = jnp.concatenate(
        [p_owner.reshape(item_count, 1), p_sub.reshape(item_count, 1),
         ap_cslot.reshape(item_count, TAP)], axis=1
    ).astype(jnp.float32)
    meta_tile = jnp.pad(meta_local.reshape(-1), (0, tile_len - item_count * (TAP + 2)))
    p2 = p_vals.reshape(item_count, HALF, LANES)
    sent = jnp.concatenate([p2, meta_tile.reshape(1, HALF, LANES)], axis=0)
    panel2 = lax.all_gather(sent, "row", axis=0, tiled=True)
    meta_all = panel2.reshape(row_devices, item_count + 1, tile_len)[:, item_count, :item_count * (TAP + 2)]
    a_split = (
        a_vals.reshape(capacity, BLOCK, HALF, 2).transpose(0, 1, 3, 2).reshape(capacity, BLOCK, BLOCK)
    )
    partial_value = ap_partial(
        a_split, a_row.reshape(capacity), a_col.reshape(capacity),
        a_slot.reshape(branches * capacity), a_count.reshape(1), panel2,
        rows_dev * row_devices, branches, group_rows
    )
    ap_rows = lax.psum_scatter(
        partial_value.reshape(group_rows, TAP, HALF, LANES), "col", scatter_dimension=0, tiled=True
    )

    owners = p_owner.reshape(item_count)
    serial = jnp.arange(item_count, dtype=jnp.int32)
    earlier = (owners[:, None] == owners[None, :]) & (serial[None, :] < serial[:, None])
    placed = owners * per_peer + jnp.sum(earlier.astype(jnp.int32), axis=1)
    slot_ids = jnp.arange(slots_total, dtype=jnp.int32)
    hit = placed[None, :] == slot_ids[:, None]
    source = jnp.where(
        jnp.any(hit, axis=1), jnp.sum(jnp.where(hit, serial[None, :], 0), axis=1), item_count
    )
    by_rank = source.reshape(row_devices, per_peer)
    incoming = []
    for k in range(per_peer):
        outgoing = contributions(by_rank[:, k], p2, ap_rows, row_devices)
        incoming.append(lax.all_to_all(outgoing, "row", split_axis=0, concat_axis=0, tiled=True))
    incoming = jnp.stack(incoming, axis=1)

    me = lax.axis_index("row").astype(jnp.float32)
    meta_all = meta_all.reshape(row_devices, item_count, TAP + 2)
    match = meta_all[:, :, 0] == me
    rank = jnp.cumsum(match.astype(jnp.int32), axis=1) - 1
    ranks = jnp.arange(per_peer, dtype=jnp.int32)
    pick = match[:, None, :] & (rank[:, None, :] == ranks[None, :, None])
    dest = meta_all[:, :, 1:2] * TC + meta_all[:, :, 2:]
    dest_slot = jnp.sum(jnp.where(pick[..., None], dest[:, None, :, :], 0.0), axis=2)
    valid = jnp.any(pick, axis=2)
    dest_slot = jnp.where(valid[..., None], dest_slot, -1.0).reshape(slots_total * TAP)
    group_coarse = col_devices * TC
    onehot = (
        dest_slot[:, None] == jnp.arange(group_coarse, dtype=jnp.float32)[None, :]
    ).astype(jnp.float32)
    coarse_part = jnp.einsum("ec,eml->cml", onehot, incoming.reshape(slots_total * TAP, HALF, LANES),
                             precision=lax.Precision.HIGH)
    coarse = lax.psum_scatter(
        coarse_part.reshape(col_devices, TC, HALF, LANES), "col", scatter_dimension=0, tiled=True
    )
    coarse = coarse.reshape(1, TC, tile_len)
    return coarse


def solution(mesh):
    placed = (
        P("row", "col", None, None),
        P("row", "col", None),
        P("row", "col", None),
        P("row", "col", None, None),
        P("row", "col"),
        P(("row", "col"), None, None),
        P(("row", "col"), None),
        P(("row", "col"), None),
        P(("row", "col"), None, None),
    )
    return jax.shard_map(
        on_device,
        mesh=mesh,
        in_specs=placed,
        out_specs=P(("row", "col"), None, None),
        check_vma=False,
    )
```

```python
import jax
import jax.numpy as jnp
from jax import lax
from jax.experimental import pallas as pl
from jax.experimental.pallas import tpu as pltpu
from jax.sharding import PartitionSpec as P

BLOCK = 64
TAP = 6
TC = 27
LANES = 128
RPD = 8
HALF = BLOCK * BLOCK // LANES

highest = lax.Precision.HIGHEST
chunk = 64


def unpack(x):
    return jnp.concatenate([x[:, :BLOCK], pltpu.roll(x, BLOCK, 1)[:, :BLOCK]], axis=0)


def ap_kernel(rows_ref, cols_ref, slots_ref, cnt_ref, a_ref, p2_ref, o_ref, p_scr, acc):
    c = pl.program_id(0)
    capacity = rows_ref.shape[0]
    cols, branches = p_scr.shape[:2]
    per_peer_tiles = p2_ref.shape[0] // (cols // RPD)

    @pl.when(c == 0)
    def _():
        acc[...] = jnp.zeros(acc.shape, acc.dtype)

        def unpack(k, carry):
            col = k // branches
            s = k % branches
            x = p2_ref[(col // RPD) * per_peer_tiles + (col % RPD) * branches + s]
            p_scr[col, s, pl.ds(0, HALF, stride=2), :] = x[:, :BLOCK]
            p_scr[col, s, pl.ds(1, HALF, stride=2), :] = pltpu.roll(x, BLOCK, 1)[:, :BLOCK]
            return carry

        lax.fori_loop(0, cols * branches, unpack, 0, unroll=8)

    count = cnt_ref[0]

    def body(u, carry):
        t = c * chunk + u
        live = t < count
        a = unpack(a_ref[u])
        col = cols_ref[t]
        row = rows_ref[t]
        for s in range(branches):
            prod = jnp.dot(
                a, p_scr[col, s], preferred_element_type=jnp.float32, precision=lax.Precision.HIGH
            )
            idx = row * TAP + slots_ref[s * capacity + t]
            acc[idx] += jnp.where(live, prod, 0.0)
        return carry

    @pl.when(c * chunk < count)
    def _():
        lax.fori_loop(0, chunk, body, 0, unroll=True)

    @pl.when(c == pl.num_programs(0) - 1)
    def _():
        def pack(i, carry):
            o_ref[i] = jnp.concatenate([acc[i, :HALF, :], acc[i, HALF:, :]], axis=1)
            return carry

        lax.fori_loop(0, acc.shape[0], pack, 0, unroll=8)


def ap_partial(tiles, rows, cols, slots, count, panel2, ncols, branches, out_rows):
    capacity = tiles.shape[0]
    chunks = capacity // chunk

    def a_map(c, rows_ref, cols_ref, slots_ref, cnt_ref):
        last = (cnt_ref[0] - 1) // chunk
        return (jnp.minimum(c, last), 0, 0)

    grid_spec = pltpu.PrefetchScalarGridSpec(
        num_scalar_prefetch=4,
        grid=(chunks,),
        in_specs=[
            pl.BlockSpec((chunk, HALF, LANES), a_map),
            pl.BlockSpec(memory_space=pltpu.VMEM),
        ],
        out_specs=pl.BlockSpec(memory_space=pltpu.VMEM),
        scratch_shapes=[
            pltpu.VMEM((ncols, branches, BLOCK, BLOCK), jnp.float32),
            pltpu.VMEM((out_rows * TAP, BLOCK, BLOCK), jnp.float32),
        ],
    )
    return pl.pallas_call(
        ap_kernel,
        out_shape=jax.ShapeDtypeStruct((out_rows * TAP, HALF, LANES), jnp.float32),
        grid_spec=grid_spec,
        compiler_params=pltpu.CompilerParams(
            dimension_semantics=("arbitrary",), vmem_limit_bytes=60 * 1024 * 1024
        ),
    )(rows, cols, slots, count, tiles, panel2)


def contrib_kernel(src_ref, p2_ref, ap2_ref, o_ref, scr):
    slots = o_ref.shape[0]
    items = p2_ref.shape[0]
    branches = items // ap2_ref.shape[0]

    def body(e, carry):
        item = src_ref[e]

        @pl.when(item < items)
        def _():
            left = unpack(p2_ref[item]).T
            for q in range(TAP):
                right = unpack(ap2_ref[item // branches, q])
                scr[...] = jnp.dot(
                    left, right, preferred_element_type=jnp.float32, precision=lax.Precision.HIGH
                )
                even = scr[pl.ds(0, HALF, stride=2), :]
                odd = scr[pl.ds(1, HALF, stride=2), :]
                o_ref[e, q] = jnp.concatenate([even, odd], axis=1)

        @pl.when(item >= items)
        def _():
            o_ref[e] = jnp.zeros(o_ref.shape[1:], o_ref.dtype)

        return carry

    lax.fori_loop(0, slots, body, 0)


def contributions(source, p2, ap2, slots):
    return pl.pallas_call(
        contrib_kernel,
        out_shape=jax.ShapeDtypeStruct((slots, TAP, HALF, LANES), jnp.float32),
        grid_spec=pltpu.PrefetchScalarGridSpec(
            num_scalar_prefetch=1,
            grid=(1,),
            in_specs=[
                pl.BlockSpec(memory_space=pltpu.VMEM),
                pl.BlockSpec(memory_space=pltpu.VMEM),
            ],
            out_specs=pl.BlockSpec(memory_space=pltpu.VMEM),
            scratch_shapes=[pltpu.VMEM((BLOCK, BLOCK), jnp.float32)],
        ),
    )(source, p2, ap2)


def on_device(a_vals, a_row, a_col, a_slot, a_count, p_vals, p_owner, p_sub, ap_cslot):
    row_devices = lax.axis_size("row")
    col_devices = lax.axis_size("col")
    capacity = a_vals.shape[2]
    rows_dev = p_vals.shape[0]
    branches = p_vals.shape[1]
    tile_len = p_vals.shape[2]
    group_rows = rows_dev * col_devices
    per_peer = 2
    item_count = rows_dev * branches
    slots_total = row_devices * per_peer

    meta_local = jnp.concatenate(
        [p_owner.reshape(item_count, 1), p_sub.reshape(item_count, 1),
         ap_cslot.reshape(item_count, TAP)], axis=1
    ).astype(jnp.float32)
    meta_tile = jnp.pad(meta_local.reshape(-1), (0, tile_len - item_count * (TAP + 2)))
    p2 = p_vals.reshape(item_count, HALF, LANES)
    sent = jnp.concatenate([p2, meta_tile.reshape(1, HALF, LANES)], axis=0)
    panel2 = lax.all_gather(sent, "row", axis=0, tiled=True)
    meta_all = panel2.reshape(row_devices, item_count + 1, tile_len)[:, item_count, :item_count * (TAP + 2)]
    a_split = a_vals.reshape(capacity, HALF, LANES)
    partial_value = ap_partial(
        a_split, a_row.reshape(capacity), a_col.reshape(capacity),
        a_slot.reshape(branches * capacity), a_count.reshape(1), panel2,
        rows_dev * row_devices, branches, group_rows
    )
    ap_rows = lax.psum_scatter(
        partial_value.reshape(group_rows, TAP, HALF, LANES), "col", scatter_dimension=0, tiled=True
    )

    owners = p_owner.reshape(item_count)
    serial = jnp.arange(item_count, dtype=jnp.int32)
    earlier = (owners[:, None] == owners[None, :]) & (serial[None, :] < serial[:, None])
    placed = owners * per_peer + jnp.sum(earlier.astype(jnp.int32), axis=1)
    slot_ids = jnp.arange(slots_total, dtype=jnp.int32)
    hit = placed[None, :] == slot_ids[:, None]
    source = jnp.where(
        jnp.any(hit, axis=1), jnp.sum(jnp.where(hit, serial[None, :], 0), axis=1), item_count
    )
    by_rank = source.reshape(row_devices, per_peer)
    incoming = []
    for k in range(per_peer):
        outgoing = contributions(by_rank[:, k], p2, ap_rows, row_devices)
        incoming.append(lax.all_to_all(outgoing, "row", split_axis=0, concat_axis=0, tiled=True))
    incoming = jnp.stack(incoming, axis=1)

    me = lax.axis_index("row").astype(jnp.float32)
    meta_all = meta_all.reshape(row_devices, item_count, TAP + 2)
    match = meta_all[:, :, 0] == me
    rank = jnp.cumsum(match.astype(jnp.int32), axis=1) - 1
    ranks = jnp.arange(per_peer, dtype=jnp.int32)
    pick = match[:, None, :] & (rank[:, None, :] == ranks[None, :, None])
    dest = meta_all[:, :, 1:2] * TC + meta_all[:, :, 2:]
    dest_slot = jnp.sum(jnp.where(pick[..., None], dest[:, None, :, :], 0.0), axis=2)
    valid = jnp.any(pick, axis=2)
    dest_slot = jnp.where(valid[..., None], dest_slot, -1.0).reshape(slots_total * TAP)
    group_coarse = col_devices * TC
    onehot = (
        dest_slot[:, None] == jnp.arange(group_coarse, dtype=jnp.float32)[None, :]
    ).astype(jnp.float32)
    coarse_part = jnp.einsum("ec,eml->cml", onehot, incoming.reshape(slots_total * TAP, HALF, LANES),
                             precision=lax.Precision.HIGH)
    coarse = lax.psum_scatter(
        coarse_part.reshape(col_devices, TC, HALF, LANES), "col", scatter_dimension=0, tiled=True
    )
    coarse = coarse.reshape(1, TC, tile_len)
    return coarse


def solution(mesh):
    placed = (
        P("row", "col", None, None),
        P("row", "col", None),
        P("row", "col", None),
        P("row", "col", None, None),
        P("row", "col"),
        P(("row", "col"), None, None),
        P(("row", "col"), None),
        P(("row", "col"), None),
        P(("row", "col"), None, None),
    )
    return jax.shard_map(
        on_device,
        mesh=mesh,
        in_specs=placed,
        out_specs=P(("row", "col"), None, None),
        check_vma=False,
    )
```

```python
import jax
import jax.numpy as jnp
from jax import lax
from jax.experimental import pallas as pl
from jax.experimental.pallas import tpu as pltpu
from jax.sharding import PartitionSpec as P

BLOCK = 64
TAP = 6
TC = 27
LANES = 128
RPD = 8
HALF = BLOCK * BLOCK // LANES

highest = lax.Precision.HIGHEST
chunk = 64


def ap_kernel(rows_ref, cols_ref, slots_ref, cnt_ref, a_ref, p2_ref, o_ref, p_scr, acc):
    c = pl.program_id(0)
    capacity = rows_ref.shape[0]
    cols, branches = p_scr.shape[:2]
    per_peer_tiles = p2_ref.shape[0] // (cols // RPD)

    @pl.when(c == 0)
    def _():
        acc[...] = jnp.zeros(acc.shape, acc.dtype)

        def unpack(k, carry):
            col = k // branches
            s = k % branches
            x = p2_ref[(col // RPD) * per_peer_tiles + (col % RPD) * branches + s]
            even = x[:, :BLOCK]
            odd = pltpu.roll(x, BLOCK, 1)[:, :BLOCK]
            p_scr[col, s] = jnp.concatenate([even, odd], axis=0)
            return carry

        lax.fori_loop(0, cols * branches, unpack, 0, unroll=8)

    count = cnt_ref[0]

    def body(u, carry):
        t = c * chunk + u
        live = t < count
        a = a_ref[u]
        col = cols_ref[t]
        row = rows_ref[t]
        for s in range(branches):
            prod = jnp.dot(
                a, p_scr[col, s], preferred_element_type=jnp.float32, precision=lax.Precision.HIGH
            )
            idx = row * TAP + slots_ref[s * capacity + t]
            acc[idx] += jnp.where(live, prod, 0.0)
        return carry

    @pl.when(c * chunk < count)
    def _():
        lax.fori_loop(0, chunk, body, 0, unroll=True)

    @pl.when(c == pl.num_programs(0) - 1)
    def _():
        def pack(i, carry):
            even = acc[i, pl.ds(0, HALF, stride=2), :]
            odd = acc[i, pl.ds(1, HALF, stride=2), :]
            o_ref[i] = jnp.concatenate([even, odd], axis=1)
            return carry

        lax.fori_loop(0, acc.shape[0], pack, 0, unroll=8)


def ap_partial(tiles, rows, cols, slots, count, panel2, ncols, branches, out_rows):
    capacity = tiles.shape[0]
    chunks = capacity // chunk

    def a_map(c, rows_ref, cols_ref, slots_ref, cnt_ref):
        last = (cnt_ref[0] - 1) // chunk
        return (jnp.minimum(c, last), 0, 0)

    grid_spec = pltpu.PrefetchScalarGridSpec(
        num_scalar_prefetch=4,
        grid=(chunks,),
        in_specs=[
            pl.BlockSpec((chunk, BLOCK, BLOCK), a_map),
            pl.BlockSpec(memory_space=pltpu.VMEM),
        ],
        out_specs=pl.BlockSpec(memory_space=pltpu.VMEM),
        scratch_shapes=[
            pltpu.VMEM((ncols, branches, BLOCK, BLOCK), jnp.float32),
            pltpu.VMEM((out_rows * TAP, BLOCK, BLOCK), jnp.float32),
        ],
    )
    return pl.pallas_call(
        ap_kernel,
        out_shape=jax.ShapeDtypeStruct((out_rows * TAP, HALF, LANES), jnp.float32),
        grid_spec=grid_spec,
        compiler_params=pltpu.CompilerParams(
            dimension_semantics=("arbitrary",), vmem_limit_bytes=60 * 1024 * 1024
        ),
    )(rows, cols, slots, count, tiles, panel2)


def unpack(x):
    return jnp.concatenate([x[:, :BLOCK], pltpu.roll(x, BLOCK, 1)[:, :BLOCK]], axis=0)


def contrib_kernel(src_ref, p2_ref, ap2_ref, o_ref, scr):
    slots = o_ref.shape[0]
    items = p2_ref.shape[0]
    branches = items // ap2_ref.shape[0]

    def body(e, carry):
        item = src_ref[e]

        @pl.when(item < items)
        def _():
            left = unpack(p2_ref[item]).T
            for q in range(TAP):
                right = unpack(ap2_ref[item // branches, q])
                scr[...] = jnp.dot(
                    left, right, preferred_element_type=jnp.float32, precision=lax.Precision.HIGH
                )
                even = scr[pl.ds(0, HALF, stride=2), :]
                odd = scr[pl.ds(1, HALF, stride=2), :]
                o_ref[e, q] = jnp.concatenate([even, odd], axis=1)

        @pl.when(item >= items)
        def _():
            o_ref[e] = jnp.zeros(o_ref.shape[1:], o_ref.dtype)

        return carry

    lax.fori_loop(0, slots, body, 0)


def contributions(source, p2, ap2, slots):
    return pl.pallas_call(
        contrib_kernel,
        out_shape=jax.ShapeDtypeStruct((slots, TAP, HALF, LANES), jnp.float32),
        grid_spec=pltpu.PrefetchScalarGridSpec(
            num_scalar_prefetch=1,
            grid=(1,),
            in_specs=[
                pl.BlockSpec(memory_space=pltpu.VMEM),
                pl.BlockSpec(memory_space=pltpu.VMEM),
            ],
            out_specs=pl.BlockSpec(memory_space=pltpu.VMEM),
            scratch_shapes=[pltpu.VMEM((BLOCK, BLOCK), jnp.float32)],
        ),
    )(source, p2, ap2)


def on_device(a_vals, a_row, a_col, a_slot, a_count, p_vals, p_owner, p_sub, ap_cslot):
    row_devices = lax.axis_size("row")
    col_devices = lax.axis_size("col")
    capacity = a_vals.shape[2]
    rows_dev = p_vals.shape[0]
    branches = p_vals.shape[1]
    tile_len = p_vals.shape[2]
    group_rows = rows_dev * col_devices
    per_peer = 2
    item_count = rows_dev * branches
    slots_total = row_devices * per_peer

    meta_local = jnp.concatenate(
        [p_owner.reshape(item_count, 1), p_sub.reshape(item_count, 1),
         ap_cslot.reshape(item_count, TAP)], axis=1
    ).astype(jnp.float32)
    meta_tile = jnp.pad(meta_local.reshape(-1), (0, tile_len - item_count * (TAP + 2)))
    p2 = p_vals.reshape(item_count, HALF, LANES)
    sent = jnp.concatenate([p2, meta_tile.reshape(1, HALF, LANES)], axis=0)
    panel2 = lax.all_gather(sent, "row", axis=0, tiled=True)
    meta_all = panel2.reshape(row_devices, item_count + 1, tile_len)[:, item_count, :item_count * (TAP + 2)]
    a_split = (
        a_vals.reshape(capacity, BLOCK, HALF, 2).transpose(0, 1, 3, 2).reshape(capacity, BLOCK, BLOCK)
    )
    partial_value = ap_partial(
        a_split, a_row.reshape(capacity), a_col.reshape(capacity),
        a_slot.reshape(branches * capacity), a_count.reshape(1), panel2,
        rows_dev * row_devices, branches, group_rows
    )
    ap_rows = lax.psum_scatter(
        partial_value.reshape(group_rows, TAP, HALF, LANES), "col", scatter_dimension=0, tiled=True
    )

    owners = p_owner.reshape(item_count)
    serial = jnp.arange(item_count, dtype=jnp.int32)
    earlier = (owners[:, None] == owners[None, :]) & (serial[None, :] < serial[:, None])
    placed = owners * per_peer + jnp.sum(earlier.astype(jnp.int32), axis=1)
    slot_ids = jnp.arange(slots_total, dtype=jnp.int32)
    hit = placed[None, :] == slot_ids[:, None]
    source = jnp.where(
        jnp.any(hit, axis=1), jnp.sum(jnp.where(hit, serial[None, :], 0), axis=1), item_count
    )
    outgoing = contributions(source, p2, ap_rows, slots_total)
    incoming = lax.all_to_all(outgoing, "row", split_axis=0, concat_axis=0, tiled=True)

    me = lax.axis_index("row").astype(jnp.float32)
    meta_all = meta_all.reshape(row_devices, item_count, TAP + 2)
    match = meta_all[:, :, 0] == me
    rank = jnp.cumsum(match.astype(jnp.int32), axis=1) - 1
    ranks = jnp.arange(per_peer, dtype=jnp.int32)
    pick = match[:, None, :] & (rank[:, None, :] == ranks[None, :, None])
    dest = meta_all[:, :, 1:2] * TC + meta_all[:, :, 2:]
    dest_slot = jnp.sum(jnp.where(pick[..., None], dest[:, None, :, :], 0.0), axis=2)
    valid = jnp.any(pick, axis=2)
    dest_slot = jnp.where(valid[..., None], dest_slot, -1.0).reshape(slots_total * TAP)
    group_coarse = col_devices * TC
    onehot = (
        dest_slot[:, None] == jnp.arange(group_coarse, dtype=jnp.float32)[None, :]
    ).astype(jnp.float32)
    coarse_part = jnp.einsum("ec,eml->cml", onehot, incoming.reshape(slots_total * TAP, HALF, LANES),
                             precision=lax.Precision.HIGH)
    coarse = lax.psum_scatter(
        coarse_part.reshape(col_devices, TC, HALF, LANES), "col", scatter_dimension=0, tiled=True
    )
    coarse = coarse.reshape(1, TC, tile_len)
    return coarse


def solution(mesh):
    placed = (
        P("row", "col", None, None),
        P("row", "col", None),
        P("row", "col", None),
        P("row", "col", None, None),
        P("row", "col"),
        P(("row", "col"), None, None),
        P(("row", "col"), None),
        P(("row", "col"), None),
        P(("row", "col"), None, None),
    )
    return jax.shard_map(
        on_device,
        mesh=mesh,
        in_specs=placed,
        out_specs=P(("row", "col"), None, None),
        check_vma=False,
    )
```

```python
import jax
import jax.numpy as jnp
from jax import lax
from jax.experimental import pallas as pl
from jax.experimental.pallas import tpu as pltpu
from jax.sharding import PartitionSpec as P

BLOCK = 64
TAP = 6
TC = 27
LANES = 128
RPD = 8
HALF = BLOCK * BLOCK // LANES

highest = lax.Precision.HIGHEST
chunk = 64


def ap_kernel(rows_ref, cols_ref, slots_ref, cnt_ref, a_ref, p2_ref, o_ref, p_scr, acc):
    c = pl.program_id(0)
    capacity = rows_ref.shape[0]
    cols, branches = p_scr.shape[:2]
    per_peer_tiles = p2_ref.shape[0] // (cols // RPD)

    @pl.when(c == 0)
    def _():
        acc[...] = jnp.zeros(acc.shape, acc.dtype)

        def unpack(k, carry):
            col = k // branches
            s = k % branches
            x = p2_ref[(col // RPD) * per_peer_tiles + (col % RPD) * branches + s]
            even = x[:, :BLOCK]
            odd = pltpu.roll(x, BLOCK, 1)[:, :BLOCK]
            p_scr[col, s] = jnp.concatenate([even, odd], axis=0)
            return carry

        lax.fori_loop(0, cols * branches, unpack, 0, unroll=8)

    count = cnt_ref[0]

    def body(u, carry):
        t = c * chunk + u
        live = t < count
        a = a_ref[u]
        col = cols_ref[t]
        row = rows_ref[t]
        for s in range(branches):
            prod = jnp.dot(
                a, p_scr[col, s], preferred_element_type=jnp.float32, precision=lax.Precision.HIGH
            )
            idx = row * TAP + slots_ref[s * capacity + t]
            acc[idx] += jnp.where(live, prod, 0.0)
        return carry

    @pl.when(c * chunk < count)
    def _():
        lax.fori_loop(0, chunk, body, 0, unroll=True)

    @pl.when(c == pl.num_programs(0) - 1)
    def _():
        def pack(i, carry):
            even = acc[i, pl.ds(0, HALF, stride=2), :]
            odd = acc[i, pl.ds(1, HALF, stride=2), :]
            o_ref[i] = jnp.concatenate([even, odd], axis=1)
            return carry

        lax.fori_loop(0, acc.shape[0], pack, 0, unroll=8)


def ap_partial(tiles, rows, cols, slots, count, panel2, ncols, branches, out_rows):
    capacity = tiles.shape[0]
    chunks = capacity // chunk

    def a_map(c, rows_ref, cols_ref, slots_ref, cnt_ref):
        last = (cnt_ref[0] - 1) // chunk
        return (jnp.minimum(c, last), 0, 0)

    grid_spec = pltpu.PrefetchScalarGridSpec(
        num_scalar_prefetch=4,
        grid=(chunks,),
        in_specs=[
            pl.BlockSpec((chunk, BLOCK, BLOCK), a_map),
            pl.BlockSpec(memory_space=pltpu.VMEM),
        ],
        out_specs=pl.BlockSpec(memory_space=pltpu.VMEM),
        scratch_shapes=[
            pltpu.VMEM((ncols, branches, BLOCK, BLOCK), jnp.float32),
            pltpu.VMEM((out_rows * TAP, BLOCK, BLOCK), jnp.float32),
        ],
    )
    return pl.pallas_call(
        ap_kernel,
        out_shape=jax.ShapeDtypeStruct((out_rows * TAP, HALF, LANES), jnp.float32),
        grid_spec=grid_spec,
        compiler_params=pltpu.CompilerParams(
            dimension_semantics=("arbitrary",), vmem_limit_bytes=60 * 1024 * 1024
        ),
    )(rows, cols, slots, count, tiles, panel2)


def unpack(x):
    return jnp.concatenate([x[:, :BLOCK], pltpu.roll(x, BLOCK, 1)[:, :BLOCK]], axis=0)


def contrib_kernel(src_ref, p2_ref, ap2_ref, o_ref, scr):
    slots = o_ref.shape[0]
    items = p2_ref.shape[0]
    branches = items // ap2_ref.shape[0]

    def body(e, carry):
        item = src_ref[e]

        @pl.when(item < items)
        def _():
            left = unpack(p2_ref[item]).T
            for q in range(TAP):
                right = unpack(ap2_ref[item // branches, q])
                scr[...] = jnp.dot(
                    left, right, preferred_element_type=jnp.float32, precision=lax.Precision.HIGH
                )
                even = scr[pl.ds(0, HALF, stride=2), :]
                odd = scr[pl.ds(1, HALF, stride=2), :]
                o_ref[e, q] = jnp.concatenate([even, odd], axis=1)

        @pl.when(item >= items)
        def _():
            o_ref[e] = jnp.zeros(o_ref.shape[1:], o_ref.dtype)

        return carry

    lax.fori_loop(0, slots, body, 0)


def contributions(source, p2, ap2, slots):
    return pl.pallas_call(
        contrib_kernel,
        out_shape=jax.ShapeDtypeStruct((slots, TAP, HALF, LANES), jnp.float32),
        grid_spec=pltpu.PrefetchScalarGridSpec(
            num_scalar_prefetch=1,
            grid=(1,),
            in_specs=[
                pl.BlockSpec(memory_space=pltpu.VMEM),
                pl.BlockSpec(memory_space=pltpu.VMEM),
            ],
            out_specs=pl.BlockSpec(memory_space=pltpu.VMEM),
            scratch_shapes=[pltpu.VMEM((BLOCK, BLOCK), jnp.float32)],
        ),
    )(source, p2, ap2)


def on_device(a_vals, a_row, a_col, a_slot, a_count, p_vals, p_owner, p_sub, ap_cslot):
    row_devices = lax.axis_size("row")
    col_devices = lax.axis_size("col")
    capacity = a_vals.shape[2]
    rows_dev = p_vals.shape[0]
    branches = p_vals.shape[1]
    tile_len = p_vals.shape[2]
    group_rows = rows_dev * col_devices
    per_peer = 2
    item_count = rows_dev * branches
    slots_total = row_devices * per_peer

    meta_local = jnp.concatenate(
        [p_owner.reshape(item_count, 1), p_sub.reshape(item_count, 1),
         ap_cslot.reshape(item_count, TAP)], axis=1
    ).astype(jnp.float32)
    meta_tile = jnp.pad(meta_local.reshape(-1), (0, tile_len - item_count * (TAP + 2)))
    p2 = p_vals.reshape(item_count, HALF, LANES)
    sent = jnp.concatenate([p2, meta_tile.reshape(1, HALF, LANES)], axis=0)
    panel2 = lax.all_gather(sent, "row", axis=0, tiled=True)
    meta_all = panel2.reshape(row_devices, item_count + 1, tile_len)[:, item_count, :item_count * (TAP + 2)]
    a_split = (
        a_vals.reshape(capacity, BLOCK, HALF, 2).transpose(0, 1, 3, 2).reshape(capacity, BLOCK, BLOCK)
    )
    partial_value = ap_partial(
        a_split, a_row.reshape(capacity), a_col.reshape(capacity),
        a_slot.reshape(branches * capacity), a_count.reshape(1), panel2,
        rows_dev * row_devices, branches, group_rows
    )
    ap_rows = lax.psum_scatter(
        partial_value.reshape(group_rows, TAP, HALF, LANES), "col", scatter_dimension=0, tiled=True
    )

    owners = p_owner.reshape(item_count)
    serial = jnp.arange(item_count, dtype=jnp.int32)
    earlier = (owners[:, None] == owners[None, :]) & (serial[None, :] < serial[:, None])
    placed = owners * per_peer + jnp.sum(earlier.astype(jnp.int32), axis=1)
    slot_ids = jnp.arange(slots_total, dtype=jnp.int32)
    hit = placed[None, :] == slot_ids[:, None]
    source = jnp.where(
        jnp.any(hit, axis=1), jnp.sum(jnp.where(hit, serial[None, :], 0), axis=1), item_count
    )
    by_rank = source.reshape(row_devices, per_peer)
    incoming = []
    for k in range(per_peer):
        outgoing = contributions(by_rank[:, k], p2, ap_rows, row_devices)
        incoming.append(lax.all_to_all(outgoing, "row", split_axis=0, concat_axis=0, tiled=True))

    me = lax.axis_index("row").astype(jnp.float32)
    meta_all = meta_all.reshape(row_devices, item_count, TAP + 2)
    match = meta_all[:, :, 0] == me
    rank = jnp.cumsum(match.astype(jnp.int32), axis=1) - 1
    ranks = jnp.arange(per_peer, dtype=jnp.int32)
    pick = match[:, None, :] & (rank[:, None, :] == ranks[None, :, None])
    dest = meta_all[:, :, 1:2] * TC + meta_all[:, :, 2:]
    dest_slot = jnp.sum(jnp.where(pick[..., None], dest[:, None, :, :], 0.0), axis=2)
    valid = jnp.any(pick, axis=2)
    dest_slot = jnp.where(valid[..., None], dest_slot, -1.0)
    group_coarse = col_devices * TC
    coarse_part = None
    for k in range(per_peer):
        onehot = (
            dest_slot[:, k].reshape(row_devices * TAP, 1)
            == jnp.arange(group_coarse, dtype=jnp.float32)[None, :]
        ).astype(jnp.float32)
        part = jnp.einsum(
            "ec,eml->cml", onehot, incoming[k].reshape(row_devices * TAP, HALF, LANES),
            precision=lax.Precision.HIGH,
        )
        coarse_part = part if coarse_part is None else coarse_part + part
    coarse = lax.psum_scatter(
        coarse_part.reshape(col_devices, TC, HALF, LANES), "col", scatter_dimension=0, tiled=True
    )
    coarse = coarse.reshape(1, TC, tile_len)
    return coarse


def solution(mesh):
    placed = (
        P("row", "col", None, None),
        P("row", "col", None),
        P("row", "col", None),
        P("row", "col", None, None),
        P("row", "col"),
        P(("row", "col"), None, None),
        P(("row", "col"), None),
        P(("row", "col"), None),
        P(("row", "col"), None, None),
    )
    return jax.shard_map(
        on_device,
        mesh=mesh,
        in_specs=placed,
        out_specs=P(("row", "col"), None, None),
        check_vma=False,
    )
```

```python
import jax
import jax.numpy as jnp
from jax import lax
from jax.experimental import pallas as pl
from jax.experimental.pallas import tpu as pltpu
from jax.sharding import PartitionSpec as P

BLOCK = 64
TAP = 6
TC = 27
LANES = 128
RPD = 8
HALF = BLOCK * BLOCK // LANES

highest = lax.Precision.HIGHEST
chunk = 112


def ap_kernel(rows_ref, cols_ref, slots_ref, cnt_ref, a_ref, p2_ref, o_ref, p_scr, acc):
    c = pl.program_id(0)
    capacity = rows_ref.shape[0]
    cols, branches = p_scr.shape[:2]
    per_peer_tiles = p2_ref.shape[0] // (cols // RPD)

    @pl.when(c == 0)
    def _():
        acc[...] = jnp.zeros(acc.shape, acc.dtype)

        def unpack(k, carry):
            col = k // branches
            s = k % branches
            x = p2_ref[(col // RPD) * per_peer_tiles + (col % RPD) * branches + s]
            even = x[:, :BLOCK]
            odd = pltpu.roll(x, BLOCK, 1)[:, :BLOCK]
            p_scr[col, s] = jnp.concatenate([even, odd], axis=0)
            return carry

        lax.fori_loop(0, cols * branches, unpack, 0, unroll=8)

    count = cnt_ref[0]

    def body(u, carry):
        t = c * chunk + u
        live = t < count
        a = a_ref[u]
        col = cols_ref[t]
        row = rows_ref[t]
        for s in range(branches):
            prod = jnp.dot(
                a, p_scr[col, s], preferred_element_type=jnp.float32, precision=lax.Precision.HIGH
            )
            idx = row * TAP + slots_ref[s * capacity + t]
            acc[idx] += jnp.where(live, prod, 0.0)
        return carry

    @pl.when(c * chunk < count)
    def _():
        lax.fori_loop(0, chunk, body, 0, unroll=True)

    @pl.when(c == pl.num_programs(0) - 1)
    def _():
        def pack(i, carry):
            even = acc[i, pl.ds(0, HALF, stride=2), :]
            odd = acc[i, pl.ds(1, HALF, stride=2), :]
            o_ref[i] = jnp.concatenate([even, odd], axis=1)
            return carry

        lax.fori_loop(0, acc.shape[0], pack, 0, unroll=8)


def ap_partial(tiles, rows, cols, slots, count, panel2, ncols, branches, out_rows):
    capacity = tiles.shape[0]
    chunks = capacity // chunk

    def a_map(c, rows_ref, cols_ref, slots_ref, cnt_ref):
        last = (cnt_ref[0] - 1) // chunk
        return (jnp.minimum(c, last), 0, 0)

    grid_spec = pltpu.PrefetchScalarGridSpec(
        num_scalar_prefetch=4,
        grid=(chunks,),
        in_specs=[
            pl.BlockSpec((chunk, BLOCK, BLOCK), a_map),
            pl.BlockSpec(memory_space=pltpu.VMEM),
        ],
        out_specs=pl.BlockSpec(memory_space=pltpu.VMEM),
        scratch_shapes=[
            pltpu.VMEM((ncols, branches, BLOCK, BLOCK), jnp.float32),
            pltpu.VMEM((out_rows * TAP, BLOCK, BLOCK), jnp.float32),
        ],
    )
    return pl.pallas_call(
        ap_kernel,
        out_shape=jax.ShapeDtypeStruct((out_rows * TAP, HALF, LANES), jnp.float32),
        grid_spec=grid_spec,
        compiler_params=pltpu.CompilerParams(
            dimension_semantics=("arbitrary",), vmem_limit_bytes=60 * 1024 * 1024
        ),
    )(rows, cols, slots, count, tiles, panel2)


def unpack(x):
    return jnp.concatenate([x[:, :BLOCK], pltpu.roll(x, BLOCK, 1)[:, :BLOCK]], axis=0)


def contrib_kernel(src_ref, p2_ref, ap2_ref, o_ref, scr):
    slots = o_ref.shape[0]
    items = p2_ref.shape[0]
    branches = items // ap2_ref.shape[0]

    def body(e, carry):
        item = src_ref[e]

        @pl.when(item < items)
        def _():
            left = unpack(p2_ref[item]).T
            for q in range(TAP):
                right = unpack(ap2_ref[item // branches, q])
                scr[...] = jnp.dot(
                    left, right, preferred_element_type=jnp.float32, precision=lax.Precision.HIGH
                )
                even = scr[pl.ds(0, HALF, stride=2), :]
                odd = scr[pl.ds(1, HALF, stride=2), :]
                o_ref[e, q] = jnp.concatenate([even, odd], axis=1)

        @pl.when(item >= items)
        def _():
            o_ref[e] = jnp.zeros(o_ref.shape[1:], o_ref.dtype)

        return carry

    lax.fori_loop(0, slots, body, 0)


def contributions(source, p2, ap2, slots):
    return pl.pallas_call(
        contrib_kernel,
        out_shape=jax.ShapeDtypeStruct((slots, TAP, HALF, LANES), jnp.float32),
        grid_spec=pltpu.PrefetchScalarGridSpec(
            num_scalar_prefetch=1,
            grid=(1,),
            in_specs=[
                pl.BlockSpec(memory_space=pltpu.VMEM),
                pl.BlockSpec(memory_space=pltpu.VMEM),
            ],
            out_specs=pl.BlockSpec(memory_space=pltpu.VMEM),
            scratch_shapes=[pltpu.VMEM((BLOCK, BLOCK), jnp.float32)],
        ),
    )(source, p2, ap2)


def on_device(a_vals, a_row, a_col, a_slot, a_count, p_vals, p_owner, p_sub, ap_cslot):
    row_devices = lax.axis_size("row")
    col_devices = lax.axis_size("col")
    capacity = a_vals.shape[2]
    rows_dev = p_vals.shape[0]
    branches = p_vals.shape[1]
    tile_len = p_vals.shape[2]
    group_rows = rows_dev * col_devices
    per_peer = 2
    item_count = rows_dev * branches
    slots_total = row_devices * per_peer

    meta_local = jnp.concatenate(
        [p_owner.reshape(item_count, 1), p_sub.reshape(item_count, 1),
         ap_cslot.reshape(item_count, TAP)], axis=1
    ).astype(jnp.float32)
    meta_tile = jnp.pad(meta_local.reshape(-1), (0, tile_len - item_count * (TAP + 2)))
    p2 = p_vals.reshape(item_count, HALF, LANES)
    sent = jnp.concatenate([p2, meta_tile.reshape(1, HALF, LANES)], axis=0)
    panel2 = lax.all_gather(sent, "row", axis=0, tiled=True)
    meta_all = panel2.reshape(row_devices, item_count + 1, tile_len)[:, item_count, :item_count * (TAP + 2)]
    a_split = (
        a_vals.reshape(capacity, BLOCK, HALF, 2).transpose(0, 1, 3, 2).reshape(capacity, BLOCK, BLOCK)
    )
    partial_value = ap_partial(
        a_split, a_row.reshape(capacity), a_col.reshape(capacity),
        a_slot.reshape(branches * capacity), a_count.reshape(1), panel2,
        rows_dev * row_devices, branches, group_rows
    )
    ap_rows = lax.psum_scatter(
        partial_value.reshape(group_rows, TAP, HALF, LANES), "col", scatter_dimension=0, tiled=True
    )

    owners = p_owner.reshape(item_count)
    serial = jnp.arange(item_count, dtype=jnp.int32)
    earlier = (owners[:, None] == owners[None, :]) & (serial[None, :] < serial[:, None])
    placed = owners * per_peer + jnp.sum(earlier.astype(jnp.int32), axis=1)
    slot_ids = jnp.arange(slots_total, dtype=jnp.int32)
    hit = placed[None, :] == slot_ids[:, None]
    source = jnp.where(
        jnp.any(hit, axis=1), jnp.sum(jnp.where(hit, serial[None, :], 0), axis=1), item_count
    )
    by_rank = source.reshape(row_devices, per_peer)
    incoming = []
    for k in range(per_peer):
        outgoing = contributions(by_rank[:, k], p2, ap_rows, row_devices)
        incoming.append(lax.all_to_all(outgoing, "row", split_axis=0, concat_axis=0, tiled=True))
    incoming = jnp.stack(incoming, axis=1)

    me = lax.axis_index("row").astype(jnp.float32)
    meta_all = meta_all.reshape(row_devices, item_count, TAP + 2)
    match = meta_all[:, :, 0] == me
    rank = jnp.cumsum(match.astype(jnp.int32), axis=1) - 1
    ranks = jnp.arange(per_peer, dtype=jnp.int32)
    pick = match[:, None, :] & (rank[:, None, :] == ranks[None, :, None])
    dest = meta_all[:, :, 1:2] * TC + meta_all[:, :, 2:]
    dest_slot = jnp.sum(jnp.where(pick[..., None], dest[:, None, :, :], 0.0), axis=2)
    valid = jnp.any(pick, axis=2)
    dest_slot = jnp.where(valid[..., None], dest_slot, -1.0).reshape(slots_total * TAP)
    group_coarse = col_devices * TC
    onehot = (
        dest_slot[:, None] == jnp.arange(group_coarse, dtype=jnp.float32)[None, :]
    ).astype(jnp.float32)
    coarse_part = jnp.einsum("ec,eml->cml", onehot, incoming.reshape(slots_total * TAP, HALF, LANES),
                             precision=lax.Precision.HIGH)
    coarse = lax.psum_scatter(
        coarse_part.reshape(col_devices, TC, HALF, LANES), "col", scatter_dimension=0, tiled=True
    )
    coarse = coarse.reshape(1, TC, tile_len)
    return coarse


def solution(mesh):
    placed = (
        P("row", "col", None, None),
        P("row", "col", None),
        P("row", "col", None),
        P("row", "col", None, None),
        P("row", "col"),
        P(("row", "col"), None, None),
        P(("row", "col"), None),
        P(("row", "col"), None),
        P(("row", "col"), None, None),
    )
    return jax.shard_map(
        on_device,
        mesh=mesh,
        in_specs=placed,
        out_specs=P(("row", "col"), None, None),
        check_vma=False,
    )
```
